32 devices in a mesh: section: 2 (over x), seq: 16 (over z, y, core).
Axes of the slice: x: 2, y: 2, z: 4, core: 2. Of those that a mesh axis runs over, the one named last changes fastest.
Arguments:
- clips: bfloat16 [2, 16, 512, 384], P(None, 'seq'), may hold values from -6 to 6
- cotangent: bfloat16 [2, 16, 512, 384], P(None, 'seq'), may hold values from -6 to 6
- spatial_taps: float32 [2, 9, 384], P('section'), may hold values from -1 to 1
- modulation: float32 [2, 2, 2, 384], P('section'), may hold values from -1 to 1
- norm_gain: float32 [2, 384], P('section'), may hold values from 0.5 to 1.5
- w_in: bfloat16 [2, 384, 768], P('section'), may hold values from -0.3125 to 0.3125
- w_out: bfloat16 [2, 768, 384], P('section'), may hold values from -0.21875 to 0.21875
- band_taps: float32 [2, 9, 384], P('section'), may hold values from -0.8 to 0.8
Outputs:
- activations: bfloat16 [2, 2, 16, 512, 384], P('section', None, 'seq')
- input_grads: bfloat16 [2, 2, 16, 512, 384], P('section', None, 'seq')
The draws below stay inside these ranges and needn't reach their ends.
All inputs are finite; a program needn't handle non-finite values.
Results may differ from the reference program's by a relative error of at most 0.017.
Values may be sent and summed in bfloat16 or wider, within the bound.
No kernel may reach another device: no remote copies, remote signals or barrier semaphores. Data moves between devices by JAX's collectives and lax.ppermute only.
A program may use at most 64 MiB of HBM per device.

```python
import jax
import jax.numpy as jnp
from jax import lax

C = 384
E = 768
H = 32
W = 16
BAND = 9
MB = 2
HW = 512
FRAMES = 16


def shard_levels(own_key, shape, cuts, smallest, top_value):
    factor_of = 1.0
    for position, parts in cuts:
        draws = jax.random.uniform(jax.random.fold_in(jax.random.fold_in(own_key, 6), position), (parts,), jnp.float32, smallest / len(cuts), top_value / len(cuts))
        factor_of = factor_of * jnp.repeat(jnp.exp(draws), shape[position] // parts).reshape((-1,) + (1,) * (len(shape) - 1 - position))
    return factor_of


def noise(own_key, shape, scale, most, cuts=(), kind=jnp.bfloat16):
    entries = scale * jax.random.normal(own_key, shape, jnp.float32)
    if cuts:
        entries = entries * shard_levels(own_key, shape, cuts, -0.22, 0.18)
    return jnp.clip(entries, -most, most).astype(kind)


def setup_inputs(seed: int = 0) -> dict:
    seeds = jax.random.split(jax.random.key(seed), 9)
    return {
        "clips": noise(seeds[0], (MB, FRAMES, HW, C), 1.0, 6.0, ((1, 16),)),
        "cotangent": noise(seeds[1], (MB, FRAMES, HW, C), 1.0, 6.0, ((1, 16),)),
        "spatial_taps": noise(seeds[2], (2, 9, C), 0.35, 1.0, ((0, 2),), jnp.float32),
        "modulation": noise(seeds[3], (2, MB, 2, C), 0.3, 1.0, ((0, 2),), jnp.float32),
        "norm_gain": jnp.clip(1.0 + 0.1 * jax.random.normal(seeds[4], (2, C), jnp.float32), 0.5, 1.5),
        "w_in": noise(seeds[5], (2, C, E), C ** -0.5, 0.3125, ((0, 2),)),
        "w_out": noise(seeds[6], (2, E, C), E ** -0.5, 0.21875, ((0, 2),)),
        "band_taps": noise(seeds[7], (2, BAND, C), 0.25, 0.8, ((0, 2),), jnp.float32),
    }


EPSILON = 1e-06

def spatial_block(values, stencil_taps, modulate, norm_gain, w_in, w_out):
    frame_count, pixel_count, channels = values.shape
    volume = values.astype(jnp.float32).reshape(frame_count, H, W, channels)
    padded = jnp.pad(volume, ((0, 0), (1, 1), (1, 1), (0, 0)))
    stencil_sum = jnp.zeros_like(volume)
    for down_step in range(3):
        for across in range(3):
            stencil_sum = stencil_sum + stencil_taps[3 * down_step + across] * padded[:, down_step:down_step + H, across:across + W]
    stencil_sum = stencil_sum.reshape(frame_count * pixel_count, channels)
    modulated = stencil_sum * (1.0 + modulate[0]) + modulate[1]
    scaled = modulated * lax.rsqrt(lax.optimization_barrier(jnp.mean(modulated * modulated, axis=-1, keepdims=True)) + EPSILON) * norm_gain
    normed = scaled.astype(jnp.bfloat16)
    hidden = jax.nn.silu(jnp.dot(normed, w_in, preferred_element_type=jnp.float32)).astype(jnp.bfloat16)
    update = jnp.dot(hidden, w_out, preferred_element_type=jnp.float32)
    return (values.astype(jnp.float32) + update.reshape(frame_count, pixel_count, channels)).astype(jnp.bfloat16)

def band_frames(values, tap_table):
    frame_count = values.shape[0]
    reach = BAND // 2
    volume = values.astype(jnp.float32)
    padded = jnp.pad(volume, ((reach, reach), (0, 0), (0, 0)))
    total = volume
    for offset in range(BAND):
        total = total + tap_table[offset] * padded[offset:offset + frame_count]
    return total.astype(jnp.bfloat16)

def reference(clips, cotangent, spatial_taps, modulation, norm_gain, w_in, w_out, band_taps):

    def segment_apply(values, which, clip_index):
        mixed = spatial_block(values, spatial_taps[which], modulation[which, clip_index], norm_gain[which], w_in[which], w_out[which])
        return band_frames(mixed, band_taps[which])
    first_acts, second_acts, first_grads, second_grads = ([], [], [], [])
    for clip_index in range(MB):
        first_out, first_pull = jax.vjp(lambda values: segment_apply(values, 0, clip_index), clips[clip_index])
        second_out, second_pull = jax.vjp(lambda values: segment_apply(values, 1, clip_index), first_out)
        second_grad = second_pull(cotangent[clip_index])[0]
        first_grad = first_pull(second_grad)[0]
        first_acts.append(first_out)
        second_acts.append(second_out)
        first_grads.append(first_grad)
        second_grads.append(second_grad)
    activations = jnp.stack([jnp.stack(first_acts), jnp.stack(second_acts)])
    input_grads = jnp.stack([jnp.stack(first_grads), jnp.stack(second_grads)])
    return (activations, input_grads)
```

```python
import jax
import jax.numpy as jnp
from jax import lax
from jax.sharding import PartitionSpec as P

H = 32
W = 16
BAND = 9


EPSILON = 1e-06


def spatial_block(values, stencil_taps, modulate, norm_gain, w_in, w_out):
    clip_count, frame_count, pixel_count, channels = values.shape
    volume = values.astype(jnp.float32).reshape(clip_count, frame_count, H, W, channels)
    padded = jnp.pad(volume, ((0, 0), (0, 0), (1, 1), (1, 1), (0, 0)))
    stencil_sum = jnp.zeros_like(volume)
    for down_step in range(3):
        for across in range(3):
            stencil_sum = (
                stencil_sum
                + stencil_taps[3 * down_step + across]
                * padded[:, :, down_step : down_step + H, across : across + W]
            )
    stencil_sum = stencil_sum.reshape(clip_count, frame_count, pixel_count, channels)
    scale = (1.0 + modulate[:, 0])[:, None, None, :]
    shift = modulate[:, 1][:, None, None, :]
    modulated = stencil_sum * scale + shift
    scaled = (
        modulated
        * lax.rsqrt(jnp.mean(modulated * modulated, axis=-1, keepdims=True) + EPSILON)
        * norm_gain
    )
    normed = scaled.astype(jnp.bfloat16).reshape(-1, channels)
    hidden = jax.nn.silu(jnp.dot(normed, w_in, preferred_element_type=jnp.float32)).astype(
        jnp.bfloat16
    )
    update = jnp.dot(hidden, w_out, preferred_element_type=jnp.float32)
    return (values.astype(jnp.float32) + update.reshape(values.shape)).astype(jnp.bfloat16)


def band_frames(values, tap_table):
    frame_count = values.shape[1]
    reach = BAND // 2
    volume = values.astype(jnp.float32)
    padded = jnp.pad(volume, ((0, 0), (reach, reach), (0, 0), (0, 0)))
    total = volume
    for offset in range(BAND):
        total = total + tap_table[offset] * padded[:, offset : offset + frame_count]
    return total.astype(jnp.bfloat16)


def temporal(values, tap_table):
    clip_count, frame_count, pixel_count, channels = values.shape
    groups = lax.axis_size("seq")
    grouped = values.reshape(clip_count, frame_count, groups, pixel_count // groups, channels)
    pixel_view = lax.all_to_all(grouped, "seq", split_axis=2, concat_axis=1, tiled=True)
    pixel_view = pixel_view.reshape(clip_count, groups * frame_count, pixel_count // groups, channels)
    banded = band_frames(pixel_view, tap_table)
    banded = banded.reshape(clip_count, groups * frame_count, 1, pixel_count // groups, channels)
    back = lax.all_to_all(banded, "seq", split_axis=1, concat_axis=2, tiled=True)
    return back.reshape(values.shape)


def on_device(clips, cotangent, spatial_taps, modulation, norm_gain, w_in, w_out, band_taps):
    first = lax.axis_index("section") == 0
    taps, mod, gain = spatial_taps[0], modulation[0], norm_gain[0]
    weight_in, weight_out, band = w_in[0], w_out[0], band_taps[0]

    def spatial(values):
        return spatial_block(values, taps, mod, gain, weight_in, weight_out)

    first_mixed, first_pull = jax.vjp(spatial, clips)
    lead_in = jnp.where(first, first_mixed, cotangent)
    lead_taps = jnp.where(first, band, band[::-1])
    lead_out = temporal(lead_in, lead_taps)

    first_acts = lax.ppermute(lead_out, "section", perm=[(0, 1)])
    second_mixed, second_pull = jax.vjp(spatial, first_acts)
    second_grad = second_pull(lead_out)[0]

    arrived_grad = lax.ppermute(second_grad, "section", perm=[(1, 0)])
    tail_in = jnp.where(first, arrived_grad, second_mixed)
    tail_taps = jnp.where(first, band[::-1], band)
    tail_out = temporal(tail_in, tail_taps)
    first_grad = first_pull(tail_out)[0]

    activations = jnp.where(first, lead_out, tail_out)
    input_grads = jnp.where(first, first_grad, second_grad)
    return (activations[None], input_grads[None])


def solution(mesh):
    placed = (
        P(None, "seq", None, None),
        P(None, "seq", None, None),
        P("section", None, None),
        P("section", None, None, None),
        P("section", None),
        P("section", None, None),
        P("section", None, None),
        P("section", None, None),
    )
    return jax.shard_map(
        on_device,
        mesh=mesh,
        in_specs=placed,
        out_specs=(P("section", None, "seq", None, None), P("section", None, "seq", None, None)),
        check_vma=False,
    )
```

```python
import jax
import jax.numpy as jnp
from jax import lax
from jax.sharding import PartitionSpec as P

H = 32
W = 16
BAND = 9


EPSILON = 1e-06


def spatial_block(values, stencil_taps, modulate, norm_gain, w_in, w_out):
    clip_count, frame_count, pixel_count, channels = values.shape
    volume = values.astype(jnp.float32).reshape(clip_count, frame_count, H, W, channels)
    padded = jnp.pad(volume, ((0, 0), (0, 0), (1, 1), (1, 1), (0, 0)))
    stencil_sum = jnp.zeros_like(volume)
    for down_step in range(3):
        for across in range(3):
            stencil_sum = (
                stencil_sum
                + stencil_taps[3 * down_step + across]
                * padded[:, :, down_step : down_step + H, across : across + W]
            )
    stencil_sum = stencil_sum.reshape(clip_count, frame_count, pixel_count, channels)
    scale = (1.0 + modulate[:, 0])[:, None, None, :]
    shift = modulate[:, 1][:, None, None, :]
    modulated = stencil_sum * scale + shift
    scaled = (
        modulated
        * lax.rsqrt(jnp.mean(modulated * modulated, axis=-1, keepdims=True) + EPSILON)
        * norm_gain
    )
    normed = scaled.astype(jnp.bfloat16).reshape(-1, channels)
    hidden = jax.nn.silu(jnp.dot(normed, w_in, preferred_element_type=jnp.float32)).astype(
        jnp.bfloat16
    )
    update = jnp.dot(hidden, w_out, preferred_element_type=jnp.float32)
    return (values.astype(jnp.float32) + update.reshape(values.shape)).astype(jnp.bfloat16)


def band_frames(values, tap_table):
    frame_count = values.shape[1]
    reach = BAND // 2
    volume = values.astype(jnp.float32)
    padded = jnp.pad(volume, ((0, 0), (reach, reach), (0, 0), (0, 0)))
    total = volume
    for offset in range(BAND):
        total = total + tap_table[offset] * padded[:, offset : offset + frame_count]
    return total.astype(jnp.bfloat16)


def temporal(values, tap_table):
    clip_count, frame_count, pixel_count, channels = values.shape
    groups = lax.axis_size("seq")
    grouped = values.reshape(clip_count, frame_count, groups, pixel_count // groups, channels)
    pixel_view = lax.all_to_all(grouped, "seq", split_axis=2, concat_axis=1, tiled=True)
    pixel_view = pixel_view.reshape(clip_count, groups * frame_count, pixel_count // groups, channels)
    banded = band_frames(pixel_view, tap_table)
    banded = banded.reshape(clip_count, groups * frame_count, 1, pixel_count // groups, channels)
    back = lax.all_to_all(banded, "seq", split_axis=1, concat_axis=2, tiled=True)
    return back.reshape(values.shape)


def on_device(clips, cotangent, spatial_taps, modulation, norm_gain, w_in, w_out, band_taps):
    first = lax.axis_index("section") == 0
    taps, mod, gain = spatial_taps[0], modulation[0], norm_gain[0]
    weight_in, weight_out, band = w_in[0], w_out[0], band_taps[0]
    lead_taps = jnp.where(first, band, band[::-1])
    tail_taps = jnp.where(first, band[::-1], band)

    def spatial(values, clip):
        return spatial_block(values, taps, mod[clip : clip + 1], gain, weight_in, weight_out)

    acts, grads = [], []
    for clip in range(clips.shape[0]):
        first_mixed, first_pull = jax.vjp(lambda v: spatial(v, clip), clips[clip : clip + 1])
        lead_in = jnp.where(first, first_mixed, cotangent[clip : clip + 1])
        lead_out = temporal(lead_in, lead_taps)

        first_acts = lax.ppermute(lead_out, "section", perm=[(0, 1)])
        second_mixed, second_pull = jax.vjp(lambda v: spatial(v, clip), first_acts)
        second_grad = second_pull(lead_out)[0]

        arrived_grad = lax.ppermute(second_grad, "section", perm=[(1, 0)])
        tail_in = jnp.where(first, arrived_grad, second_mixed)
        tail_out = temporal(tail_in, tail_taps)
        first_grad = first_pull(tail_out)[0]

        acts.append(jnp.where(first, lead_out, tail_out))
        grads.append(jnp.where(first, first_grad, second_grad))
    return (jnp.concatenate(acts)[None], jnp.concatenate(grads)[None])


def solution(mesh):
    placed = (
        P(None, "seq", None, None),
        P(None, "seq", None, None),
        P("section", None, None),
        P("section", None, None, None),
        P("section", None),
        P("section", None, None),
        P("section", None, None),
        P("section", None, None),
    )
    return jax.shard_map(
        on_device,
        mesh=mesh,
        in_specs=placed,
        out_specs=(P("section", None, "seq", None, None), P("section", None, "seq", None, None)),
        check_vma=False,
    )
```

```python
import jax
import jax.numpy as jnp
from jax import lax
from jax.sharding import PartitionSpec as P

H = 32
W = 16
BAND = 9


EPSILON = 1e-06


def spatial_block(values, stencil_taps, modulate, norm_gain, w_in, w_out):
    clip_count, frame_count, pixel_count, channels = values.shape
    volume = values.astype(jnp.float32).reshape(clip_count, frame_count, H, W, channels)
    padded = jnp.pad(volume, ((0, 0), (0, 0), (1, 1), (1, 1), (0, 0)))
    stencil_sum = jnp.zeros_like(volume)
    for down_step in range(3):
        for across in range(3):
            stencil_sum = (
                stencil_sum
                + stencil_taps[3 * down_step + across]
                * padded[:, :, down_step : down_step + H, across : across + W]
            )
    stencil_sum = stencil_sum.reshape(clip_count, frame_count, pixel_count, channels)
    scale = (1.0 + modulate[:, 0])[:, None, None, :]
    shift = modulate[:, 1][:, None, None, :]
    modulated = stencil_sum * scale + shift
    scaled = (
        modulated
        * lax.rsqrt(jnp.mean(modulated * modulated, axis=-1, keepdims=True) + EPSILON)
        * norm_gain
    )
    normed = scaled.astype(jnp.bfloat16).reshape(-1, channels)
    hidden = jax.nn.silu(jnp.dot(normed, w_in, preferred_element_type=jnp.float32)).astype(
        jnp.bfloat16
    )
    update = jnp.dot(hidden, w_out, preferred_element_type=jnp.float32)
    return (values.astype(jnp.float32) + update.reshape(values.shape)).astype(jnp.bfloat16)


def band_frames(values, tap_table):
    frame_count = values.shape[1]
    reach = BAND // 2
    volume = values.astype(jnp.float32)
    padded = jnp.pad(volume, ((0, 0), (reach, reach), (0, 0), (0, 0)))
    total = volume
    for offset in range(BAND):
        total = total + tap_table[:, offset, None, None, :] * padded[:, offset : offset + frame_count]
    return total.astype(jnp.bfloat16)


def temporal(values, tap_table):
    clip_count, frame_count, pixel_count, channels = values.shape
    groups = lax.axis_size("seq")
    grouped = values.reshape(clip_count, frame_count, groups, pixel_count // groups, channels)
    pixel_view = lax.all_to_all(grouped, "seq", split_axis=2, concat_axis=1, tiled=True)
    pixel_view = pixel_view.reshape(clip_count, groups * frame_count, pixel_count // groups, channels)
    banded = band_frames(pixel_view, tap_table)
    banded = banded.reshape(clip_count, groups * frame_count, 1, pixel_count // groups, channels)
    back = lax.all_to_all(banded, "seq", split_axis=1, concat_axis=2, tiled=True)
    return back.reshape(values.shape)


def on_device(clips, cotangent, spatial_taps, modulation, norm_gain, w_in, w_out, band_taps):
    plane = lax.axis_index("section")
    first = plane == 0
    clip_total, channels = clips.shape[0], clips.shape[-1]
    tap_count = spatial_taps.shape[1]
    small = jnp.concatenate(
        [
            spatial_taps[0],
            modulation[0].reshape(-1, channels),
            norm_gain,
            band_taps[0],
        ]
    )
    small_all = lax.all_gather(small, "section", axis=0, tiled=False)
    in_all = lax.all_gather(w_in[0], "section", axis=0, tiled=False)
    out_all = lax.all_gather(w_out[0], "section", axis=0, tiled=False)

    def params(segment):
        table = small_all[segment]
        taps = table[:tap_count]
        mods = table[tap_count : tap_count + 2 * clip_total].reshape(clip_total, 2, channels)
        gain = table[tap_count + 2 * clip_total]
        band = table[tap_count + 2 * clip_total + 1 :]
        mod = lax.dynamic_index_in_dim(mods, plane, 0, keepdims=True)
        return taps, mod, gain, band

    taps0, mod0, gain0, band0 = params(0)
    taps1, mod1, gain1, band1 = params(1)

    def spatial0(values):
        return spatial_block(values, taps0, mod0, gain0, in_all[0], out_all[0])

    def spatial1(values):
        return spatial_block(values, taps1, mod1, gain1, in_all[1], out_all[1])

    start = lax.dynamic_index_in_dim(clips, plane, 0, keepdims=True)
    seed = lax.dynamic_index_in_dim(cotangent, plane, 0, keepdims=True)
    second_seed = temporal(seed, band1[::-1][None])

    first_mixed, first_pull = jax.vjp(spatial0, start)
    first_act = temporal(first_mixed, band0[None])
    second_mixed, second_pull = jax.vjp(spatial1, first_act)
    second_grad = second_pull(second_seed)[0]

    tail = temporal(
        jnp.concatenate([second_grad, second_mixed]), jnp.stack([band0[::-1], band1])
    )
    first_seed, second_act = tail[:1], tail[1:]

    swap = [(0, 1), (1, 0)]
    other_act = lax.ppermute(jnp.where(first, second_act, first_act), "section", perm=swap)
    first_grad = first_pull(first_seed)[0]
    other_grad = lax.ppermute(jnp.where(first, second_grad, first_grad), "section", perm=swap)

    activations = jnp.where(
        first,
        jnp.concatenate([first_act, other_act]),
        jnp.concatenate([other_act, second_act]),
    )
    input_grads = jnp.where(
        first,
        jnp.concatenate([first_grad, other_grad]),
        jnp.concatenate([other_grad, second_grad]),
    )
    return (activations[None], input_grads[None])


def solution(mesh):
    placed = (
        P(None, "seq", None, None),
        P(None, "seq", None, None),
        P("section", None, None),
        P("section", None, None, None),
        P("section", None),
        P("section", None, None),
        P("section", None, None),
        P("section", None, None),
    )
    return jax.shard_map(
        on_device,
        mesh=mesh,
        in_specs=placed,
        out_specs=(P("section", None, "seq", None, None), P("section", None, "seq", None, None)),
        check_vma=False,
    )
```

```python
import jax
import jax.numpy as jnp
from jax import lax
from jax.sharding import PartitionSpec as P

H = 32
W = 16
BAND = 9


EPSILON = 1e-06


def spatial_block(values, stencil_taps, modulate, norm_gain, w_in, w_out):
    clip_count, frame_count, pixel_count, channels = values.shape
    volume = values.astype(jnp.float32).reshape(clip_count, frame_count, H, W, channels)
    padded = jnp.pad(volume, ((0, 0), (0, 0), (1, 1), (1, 1), (0, 0)))
    stencil_sum = jnp.zeros_like(volume)
    for down_step in range(3):
        for across in range(3):
            stencil_sum = (
                stencil_sum
                + stencil_taps[3 * down_step + across]
                * padded[:, :, down_step : down_step + H, across : across + W]
            )
    stencil_sum = stencil_sum.reshape(clip_count, frame_count, pixel_count, channels)
    scale = (1.0 + modulate[:, 0])[:, None, None, :]
    shift = modulate[:, 1][:, None, None, :]
    modulated = stencil_sum * scale + shift
    scaled = (
        modulated
        * lax.rsqrt(jnp.mean(modulated * modulated, axis=-1, keepdims=True) + EPSILON)
        * norm_gain
    )
    normed = scaled.astype(jnp.bfloat16).reshape(-1, channels)
    hidden = jax.nn.silu(jnp.dot(normed, w_in, preferred_element_type=jnp.float32)).astype(
        jnp.bfloat16
    )
    update = jnp.dot(hidden, w_out, preferred_element_type=jnp.float32)
    return (values.astype(jnp.float32) + update.reshape(values.shape)).astype(jnp.bfloat16)


def band_frames(values, tap_table):
    frame_count = values.shape[1]
    reach = BAND // 2
    volume = values.astype(jnp.float32)
    padded = jnp.pad(volume, ((0, 0), (reach, reach), (0, 0), (0, 0)))
    total = volume
    for offset in range(BAND):
        total = total + tap_table[:, offset, None, None, :] * padded[:, offset : offset + frame_count]
    return total.astype(jnp.bfloat16)


def temporal(values, tap_table):
    clip_count, frame_count, pixel_count, channels = values.shape
    groups = lax.axis_size("seq")
    grouped = values.reshape(clip_count, frame_count, groups, pixel_count // groups, channels)
    pixel_view = lax.all_to_all(grouped, "seq", split_axis=2, concat_axis=1, tiled=True)
    pixel_view = pixel_view.reshape(clip_count, groups * frame_count, pixel_count // groups, channels)
    banded = band_frames(pixel_view, tap_table)
    banded = banded.reshape(clip_count, groups * frame_count, 1, pixel_count // groups, channels)
    back = lax.all_to_all(banded, "seq", split_axis=1, concat_axis=2, tiled=True)
    return back.reshape(values.shape)


def on_device(clips, cotangent, spatial_taps, modulation, norm_gain, w_in, w_out, band_taps):
    first = lax.axis_index("section") == 0
    taps, mod, gain = spatial_taps[0], modulation[0], norm_gain[0]
    weight_in, weight_out, band = w_in[0], w_out[0], band_taps[0]

    to_first = [(1, 0)]
    second_taps, second_mod, second_gain, second_in, second_out = [
        jnp.where(first, lax.ppermute(p, "section", perm=to_first), p)
        for p in (taps, mod, gain, weight_in, weight_out)
    ]

    def spatial(values):
        return spatial_block(values, taps, mod, gain, weight_in, weight_out)

    def second_spatial(values):
        return spatial_block(
            values, second_taps, second_mod, second_gain, second_in, second_out
        )

    first_mixed, first_pull = jax.vjp(spatial, clips)
    lead_in = jnp.where(first, first_mixed, cotangent)
    lead_taps = jnp.where(first, band, band[::-1])
    lead_out = temporal(lead_in, lead_taps[None])

    swapped = lax.ppermute(lead_out, "section", perm=[(0, 1), (1, 0)])
    first_acts = jnp.where(first, lead_out, swapped)
    second_seed = jnp.where(first, swapped, lead_out)
    second_mixed, second_pull = jax.vjp(second_spatial, first_acts)
    second_grad = second_pull(second_seed)[0]

    tail_in = jnp.where(first, second_grad, second_mixed)
    tail_taps = jnp.where(first, band[::-1], band)
    tail_out = temporal(tail_in, tail_taps[None])
    first_grad = first_pull(tail_out)[0]

    activations = jnp.where(first, lead_out, tail_out)
    input_grads = jnp.where(first, first_grad, second_grad)
    return (activations[None], input_grads[None])


def solution(mesh):
    placed = (
        P(None, "seq", None, None),
        P(None, "seq", None, None),
        P("section", None, None),
        P("section", None, None, None),
        P("section", None),
        P("section", None, None),
        P("section", None, None),
        P("section", None, None),
    )
    return jax.shard_map(
        on_device,
        mesh=mesh,
        in_specs=placed,
        out_specs=(P("section", None, "seq", None, None), P("section", None, "seq", None, None)),
        check_vma=False,
    )
```

```python
import jax
import jax.numpy as jnp
from jax import lax
from jax.sharding import PartitionSpec as P

H = 32
W = 16
BAND = 9


EPSILON = 1e-06


def spatial_block(values, stencil_taps, modulate, norm_gain, w_in, w_out):
    clip_count, frame_count, pixel_count, channels = values.shape
    volume = values.astype(jnp.float32).reshape(clip_count, frame_count, H, W, channels)
    padded = jnp.pad(volume, ((0, 0), (0, 0), (1, 1), (1, 1), (0, 0)))
    stencil_sum = jnp.zeros_like(volume)
    for down_step in range(3):
        for across in range(3):
            stencil_sum = (
                stencil_sum
                + stencil_taps[3 * down_step + across]
                * padded[:, :, down_step : down_step + H, across : across + W]
            )
    stencil_sum = stencil_sum.reshape(clip_count, frame_count, pixel_count, channels)
    scale = (1.0 + modulate[:, 0])[:, None, None, :]
    shift = modulate[:, 1][:, None, None, :]
    modulated = stencil_sum * scale + shift
    scaled = (
        modulated
        * lax.rsqrt(jnp.mean(modulated * modulated, axis=-1, keepdims=True) + EPSILON)
        * norm_gain
    )
    normed = scaled.astype(jnp.bfloat16).reshape(-1, channels)
    hidden = jax.nn.silu(jnp.dot(normed, w_in, preferred_element_type=jnp.float32)).astype(
        jnp.bfloat16
    )
    update = jnp.dot(hidden, w_out, preferred_element_type=jnp.float32)
    return (values.astype(jnp.float32) + update.reshape(values.shape)).astype(jnp.bfloat16)


def band_frames(values, tap_table):
    frame_count = values.shape[1]
    reach = BAND // 2
    volume = values.astype(jnp.float32)
    padded = jnp.pad(volume, ((0, 0), (reach, reach), (0, 0), (0, 0)))
    total = volume
    for offset in range(BAND):
        total = total + tap_table[:, offset, None, None, :] * padded[:, offset : offset + frame_count]
    return total.astype(jnp.bfloat16)


def temporal(values, tap_table):
    clip_count, frame_count, pixel_count, channels = values.shape
    groups = lax.axis_size("seq")
    grouped = values.reshape(clip_count, frame_count, groups, pixel_count // groups, channels)
    pixel_view = lax.all_to_all(grouped, "seq", split_axis=2, concat_axis=1, tiled=True)
    pixel_view = pixel_view.reshape(clip_count, groups * frame_count, pixel_count // groups, channels)
    banded = band_frames(pixel_view, tap_table)
    banded = banded.reshape(clip_count, groups * frame_count, 1, pixel_count // groups, channels)
    back = lax.all_to_all(banded, "seq", split_axis=1, concat_axis=2, tiled=True)
    return back.reshape(values.shape)


def on_device(clips, cotangent, spatial_taps, modulation, norm_gain, w_in, w_out, band_taps):
    first = lax.axis_index("section") == 0
    taps, mod, gain = spatial_taps[0], modulation[0], norm_gain[0]
    weight_in, weight_out, band = w_in[0], w_out[0], band_taps[0]

    to_first = [(1, 0)]
    core = lax.axis_index("seq") % 2
    siblings = [(q, q ^ 1) for q in range(lax.axis_size("seq"))]

    def fetch_halves(p):
        half = p.shape[0] // 2
        mine = lax.dynamic_slice_in_dim(p, core * half, half, 0)
        got = lax.ppermute(mine, "section", perm=to_first)
        other = lax.ppermute(got, "seq", perm=siblings)
        return jnp.where(core == 0, jnp.concatenate([got, other]), jnp.concatenate([other, got]))

    second_taps, second_mod, second_gain = [
        jnp.where(first, lax.ppermute(p, "section", perm=to_first), p)
        for p in (taps, mod, gain)
    ]
    second_in, second_out = [
        jnp.where(first, fetch_halves(p), p) for p in (weight_in, weight_out)
    ]

    def spatial(values):
        return spatial_block(values, taps, mod, gain, weight_in, weight_out)

    def second_spatial(values):
        return spatial_block(
            values, second_taps, second_mod, second_gain, second_in, second_out
        )

    first_mixed, first_pull = jax.vjp(spatial, clips)
    lead_in = jnp.where(first, first_mixed, cotangent)
    lead_taps = jnp.where(first, band, band[::-1])
    lead_out = temporal(lead_in, lead_taps[None])

    swapped = lax.ppermute(lead_out, "section", perm=[(0, 1), (1, 0)])
    first_acts = jnp.where(first, lead_out, swapped)
    second_seed = jnp.where(first, swapped, lead_out)
    second_mixed, second_pull = jax.vjp(second_spatial, first_acts)
    second_grad = second_pull(second_seed)[0]

    tail_in = jnp.where(first, second_grad, second_mixed)
    tail_taps = jnp.where(first, band[::-1], band)
    tail_out = temporal(tail_in, tail_taps[None])
    first_grad = first_pull(tail_out)[0]

    activations = jnp.where(first, lead_out, tail_out)
    input_grads = jnp.where(first, first_grad, second_grad)
    return (activations[None], input_grads[None])


def solution(mesh):
    placed = (
        P(None, "seq", None, None),
        P(None, "seq", None, None),
        P("section", None, None),
        P("section", None, None, None),
        P("section", None),
        P("section", None, None),
        P("section", None, None),
        P("section", None, None),
    )
    return jax.shard_map(
        on_device,
        mesh=mesh,
        in_specs=placed,
        out_specs=(P("section", None, "seq", None, None), P("section", None, "seq", None, None)),
        check_vma=False,
    )
```

```python
import jax
import jax.numpy as jnp
from jax import lax
from jax.sharding import PartitionSpec as P

H = 32
W = 16
BAND = 9


EPSILON = 1e-06


def spatial_block(values, stencil_taps, modulate, norm_gain, w_in, w_out):
    clip_count, frame_count, pixel_count, channels = values.shape
    volume = values.astype(jnp.float32).reshape(clip_count, frame_count, H, W, channels)
    padded = jnp.pad(volume, ((0, 0), (0, 0), (1, 1), (1, 1), (0, 0)))
    stencil_sum = jnp.zeros_like(volume)
    for down_step in range(3):
        for across in range(3):
            stencil_sum = (
                stencil_sum
                + stencil_taps[3 * down_step + across]
                * padded[:, :, down_step : down_step + H, across : across + W]
            )
    stencil_sum = stencil_sum.reshape(clip_count, frame_count, pixel_count, channels)
    scale = (1.0 + modulate[:, 0])[:, None, None, :]
    shift = modulate[:, 1][:, None, None, :]
    modulated = stencil_sum * scale + shift
    scaled = (
        modulated
        * lax.rsqrt(jnp.mean(modulated * modulated, axis=-1, keepdims=True) + EPSILON)
        * norm_gain
    )
    normed = scaled.astype(jnp.bfloat16).reshape(-1, channels)
    hidden = jax.nn.silu(jnp.dot(normed, w_in, preferred_element_type=jnp.float32)).astype(
        jnp.bfloat16
    )
    update = jnp.dot(hidden, w_out, preferred_element_type=jnp.float32)
    return (values.astype(jnp.float32) + update.reshape(values.shape)).astype(jnp.bfloat16)


def band_frames(values, tap_table):
    frame_count = values.shape[1]
    reach = BAND // 2
    volume = values.astype(jnp.float32)
    padded = jnp.pad(volume, ((0, 0), (reach, reach), (0, 0), (0, 0)))
    total = volume
    for offset in range(BAND):
        total = total + tap_table[:, offset, None, None, :] * padded[:, offset : offset + frame_count]
    return total.astype(jnp.bfloat16)


def temporal(values, tap_table):
    clip_count, frame_count, pixel_count, channels = values.shape
    groups = lax.axis_size("seq")
    grouped = values.reshape(clip_count, frame_count, groups, pixel_count // groups, channels)
    pixel_view = lax.all_to_all(grouped, "seq", split_axis=2, concat_axis=1, tiled=True)
    pixel_view = pixel_view.reshape(clip_count, groups * frame_count, pixel_count // groups, channels)
    banded = band_frames(pixel_view, tap_table)
    banded = banded.reshape(clip_count, groups * frame_count, 1, pixel_count // groups, channels)
    back = lax.all_to_all(banded, "seq", split_axis=1, concat_axis=2, tiled=True)
    return back.reshape(values.shape)


def temporal_shared(values, tap_table):
    clip_count, frame_count, pixel_count, channels = values.shape
    groups = lax.axis_size("seq")
    planes = lax.axis_size("section")
    grouped = values.reshape(clip_count, frame_count, groups, pixel_count // groups, channels)
    pixel_view = lax.all_to_all(grouped, "seq", split_axis=2, concat_axis=1, tiled=True)
    pixel_view = pixel_view.reshape(clip_count, groups * frame_count, pixel_count // groups, channels)
    banded = band_frames(pixel_view, tap_table)
    banded = jnp.broadcast_to(
        banded[:, None], (clip_count, planes) + banded.shape[1:]
    ).reshape(clip_count, planes * groups * frame_count, 1, pixel_count // groups, channels)
    back = lax.all_to_all(banded, ("section", "seq"), split_axis=1, concat_axis=2, tiled=True)
    back = back.reshape(clip_count, frame_count, planes, pixel_count, channels)
    return jnp.moveaxis(back, 2, 0)


def on_device(clips, cotangent, spatial_taps, modulation, norm_gain, w_in, w_out, band_taps):
    first = lax.axis_index("section") == 0
    taps, mod, gain = spatial_taps[0], modulation[0], norm_gain[0]
    weight_in, weight_out, band = w_in[0], w_out[0], band_taps[0]

    to_first = [(1, 0)]
    core = lax.axis_index("seq") % 2
    siblings = [(q, q ^ 1) for q in range(lax.axis_size("seq"))]

    def fetch_halves(p):
        half = p.shape[0] // 2
        mine = lax.dynamic_slice_in_dim(p, core * half, half, 0)
        got = lax.ppermute(mine, "section", perm=to_first)
        other = lax.ppermute(got, "seq", perm=siblings)
        return jnp.where(core == 0, jnp.concatenate([got, other]), jnp.concatenate([other, got]))

    second_taps, second_mod, second_gain = [
        jnp.where(first, lax.ppermute(p, "section", perm=to_first), p)
        for p in (taps, mod, gain)
    ]
    second_in, second_out = lax.optimization_barrier(
        [jnp.where(first, fetch_halves(p), p) for p in (weight_in, weight_out)]
    )

    def spatial(values):
        return spatial_block(values, taps, mod, gain, weight_in, weight_out)

    def second_spatial(values):
        return spatial_block(
            values, second_taps, second_mod, second_gain, second_in, second_out
        )

    first_mixed, first_pull = jax.vjp(spatial, clips)
    lead_in = jnp.where(first, first_mixed, cotangent)
    lead_taps = jnp.where(first, band, band[::-1])
    first_acts, second_seed = temporal_shared(lead_in, lead_taps[None])
    second_mixed, second_pull = jax.vjp(second_spatial, first_acts)
    second_grad = second_pull(second_seed)[0]

    tail_in = jnp.where(first, second_grad, second_mixed)
    tail_taps = jnp.where(first, band[::-1], band)
    tail_out = temporal(tail_in, tail_taps[None])
    first_grad = first_pull(tail_out)[0]

    activations = jnp.where(first, first_acts, tail_out)
    input_grads = jnp.where(first, first_grad, second_grad)
    return (activations[None], input_grads[None])


def solution(mesh):
    placed = (
        P(None, "seq", None, None),
        P(None, "seq", None, None),
        P("section", None, None),
        P("section", None, None, None),
        P("section", None),
        P("section", None, None),
        P("section", None, None),
        P("section", None, None),
    )
    return jax.shard_map(
        on_device,
        mesh=mesh,
        in_specs=placed,
        out_specs=(P("section", None, "seq", None, None), P("section", None, "seq", None, None)),
        check_vma=False,
    )
```

```python
import jax
import jax.numpy as jnp
from jax import lax
from jax.sharding import PartitionSpec as P

H = 32
W = 16
BAND = 9


EPSILON = 1e-06


def spatial_block(values, stencil_taps, modulate, norm_gain, w_in, w_out):
    clip_count, frame_count, pixel_count, channels = values.shape
    volume = values.astype(jnp.float32).reshape(clip_count, frame_count, H, W, channels)
    padded = jnp.pad(volume, ((0, 0), (0, 0), (1, 1), (1, 1), (0, 0)))
    stencil_sum = jnp.zeros_like(volume)
    for down_step in range(3):
        for across in range(3):
            stencil_sum = (
                stencil_sum
                + stencil_taps[3 * down_step + across]
                * padded[:, :, down_step : down_step + H, across : across + W]
            )
    stencil_sum = stencil_sum.reshape(clip_count, frame_count, pixel_count, channels)
    scale = (1.0 + modulate[:, 0])[:, None, None, :]
    shift = modulate[:, 1][:, None, None, :]
    modulated = stencil_sum * scale + shift
    scaled = (
        modulated
        * lax.rsqrt(jnp.mean(modulated * modulated, axis=-1, keepdims=True) + EPSILON)
        * norm_gain
    )
    normed = scaled.astype(jnp.bfloat16).reshape(-1, channels)
    hidden = jax.nn.silu(jnp.dot(normed, w_in, preferred_element_type=jnp.float32)).astype(
        jnp.bfloat16
    )
    update = jnp.dot(hidden, w_out, preferred_element_type=jnp.float32)
    return (values.astype(jnp.float32) + update.reshape(values.shape)).astype(jnp.bfloat16)


def band_frames(values, tap_table):
    frame_count = values.shape[1]
    reach = BAND // 2
    volume = values.astype(jnp.float32)
    padded = jnp.pad(volume, ((0, 0), (reach, reach), (0, 0), (0, 0)))
    total = volume
    for offset in range(BAND):
        total = total + tap_table[:, offset, None, None, :] * padded[:, offset : offset + frame_count]
    return total.astype(jnp.bfloat16)


def temporal(values, tap_table):
    clip_count, frame_count, pixel_count, channels = values.shape
    groups = lax.axis_size("seq")
    grouped = values.reshape(clip_count, frame_count, groups, pixel_count // groups, channels)
    pixel_view = lax.all_to_all(grouped, "seq", split_axis=2, concat_axis=1, tiled=True)
    pixel_view = pixel_view.reshape(clip_count, groups * frame_count, pixel_count // groups, channels)
    banded = band_frames(pixel_view, tap_table)
    banded = banded.reshape(clip_count, groups * frame_count, 1, pixel_count // groups, channels)
    back = lax.all_to_all(banded, "seq", split_axis=1, concat_axis=2, tiled=True)
    return back.reshape(values.shape)


def temporal_shared(values, tap_table, carried):
    clip_count, frame_count, pixel_count, channels = values.shape
    groups = lax.axis_size("seq")
    planes = lax.axis_size("section")
    grouped = values.reshape(clip_count, frame_count, groups, pixel_count // groups, channels)
    pixel_view = lax.all_to_all(grouped, "seq", split_axis=2, concat_axis=1, tiled=True)
    pixel_view, carried = lax.optimization_barrier((pixel_view, carried))
    pixel_view = pixel_view.reshape(clip_count, groups * frame_count, pixel_count // groups, channels)
    banded = band_frames(pixel_view, tap_table)
    banded = jnp.broadcast_to(
        banded[:, None], (clip_count, planes) + banded.shape[1:]
    ).reshape(clip_count, planes * groups * frame_count, 1, pixel_count // groups, channels)
    back = lax.all_to_all(banded, ("section", "seq"), split_axis=1, concat_axis=2, tiled=True)
    back = back.reshape(clip_count, frame_count, planes, pixel_count, channels)
    return jnp.moveaxis(back, 2, 0), carried


def on_device(clips, cotangent, spatial_taps, modulation, norm_gain, w_in, w_out, band_taps):
    first = lax.axis_index("section") == 0
    taps, mod, gain = spatial_taps[0], modulation[0], norm_gain[0]
    weight_in, weight_out, band = w_in[0], w_out[0], band_taps[0]

    to_first = [(1, 0)]
    core = lax.axis_index("seq") % 2
    siblings = [(q, q ^ 1) for q in range(lax.axis_size("seq"))]

    def fetch_halves(p):
        half = p.shape[0] // 2
        mine = lax.dynamic_slice_in_dim(p, core * half, half, 0)
        got = lax.ppermute(mine, "section", perm=to_first)
        other = lax.ppermute(got, "seq", perm=siblings)
        return jnp.where(core == 0, jnp.concatenate([got, other]), jnp.concatenate([other, got]))

    second_taps, second_mod, second_gain = [
        jnp.where(first, lax.ppermute(p, "section", perm=to_first), p)
        for p in (taps, mod, gain)
    ]
    second_in, second_out = [
        jnp.where(first, fetch_halves(p), p) for p in (weight_in, weight_out)
    ]

    def spatial_first(values):
        return spatial_block(values, taps, mod, gain, weight_in, weight_out)

    first_mixed, first_pull = jax.vjp(spatial_first, clips)
    lead_in = jnp.where(first, first_mixed, cotangent)
    lead_taps = jnp.where(first, band, band[::-1])
    (first_acts, second_seed), second_params = temporal_shared(
        lead_in, lead_taps[None], (second_taps, second_mod, second_gain, second_in, second_out)
    )

    def second_spatial(values):
        return spatial_block(values, *second_params)

    second_mixed, second_pull = jax.vjp(second_spatial, first_acts)
    second_grad = second_pull(second_seed)[0]

    tail_in = jnp.where(first, second_grad, second_mixed)
    tail_taps = jnp.where(first, band[::-1], band)
    tail_out = temporal(tail_in, tail_taps[None])
    first_grad = first_pull(tail_out)[0]

    activations = jnp.where(first, first_acts, tail_out)
    input_grads = jnp.where(first, first_grad, second_grad)
    return (activations[None], input_grads[None])


def solution(mesh):
    placed = (
        P(None, "seq", None, None),
        P(None, "seq", None, None),
        P("section", None, None),
        P("section", None, None, None),
        P("section", None),
        P("section", None, None),
        P("section", None, None),
        P("section", None, None),
    )
    return jax.shard_map(
        on_device,
        mesh=mesh,
        in_specs=placed,
        out_specs=(P("section", None, "seq", None, None), P("section", None, "seq", None, None)),
        check_vma=False,
    )
```

```python
import jax
import jax.numpy as jnp
from jax import lax
from jax.sharding import PartitionSpec as P

H = 32
W = 16
BAND = 9


EPSILON = 1e-06


def stencil(volume, stencil_taps):
    padded = jnp.pad(volume, ((0, 0), (0, 0), (1, 1), (1, 1), (0, 0)))
    total = jnp.zeros_like(volume)
    for down_step in range(3):
        for across in range(3):
            total = total + stencil_taps[3 * down_step + across] * padded[
                :, :, down_step : down_step + H, across : across + W
            ]
    return total


def spatial_forward(values, stencil_taps, modulate, norm_gain, w_in, w_out):
    clip_count, frame_count, pixel_count, channels = values.shape
    volume = values.astype(jnp.float32).reshape(clip_count, frame_count, H, W, channels)
    stencil_sum = stencil(volume, stencil_taps).reshape(values.shape)
    scale = (1.0 + modulate[:, 0])[:, None, None, :]
    shift = modulate[:, 1][:, None, None, :]
    modulated = stencil_sum * scale + shift
    inv_rms = lax.rsqrt(jnp.mean(modulated * modulated, axis=-1, keepdims=True) + EPSILON)
    normed = (modulated * inv_rms * norm_gain).astype(jnp.bfloat16).reshape(-1, channels)
    pre = jnp.dot(normed, w_in, preferred_element_type=jnp.float32)
    hidden = jax.nn.silu(pre).astype(jnp.bfloat16)
    update = jnp.dot(hidden, w_out, preferred_element_type=jnp.float32)
    out = (values.astype(jnp.float32) + update.reshape(values.shape)).astype(jnp.bfloat16)
    return out, (modulated, inv_rms, pre)


def spatial_backward(saved, grad, stencil_taps, modulate, norm_gain, w_in, w_out):
    modulated, inv_rms, pre = saved
    clip_count, frame_count, pixel_count, channels = grad.shape
    flat_grad = grad.reshape(-1, channels)
    hidden_grad = jnp.dot(flat_grad, w_out.T, preferred_element_type=jnp.float32).astype(jnp.bfloat16)
    gate = jax.nn.sigmoid(pre)
    pre_grad = hidden_grad.astype(jnp.float32) * (gate * (1.0 + pre * (1.0 - gate)))
    pre_grad = lax.optimization_barrier(pre_grad.astype(jnp.bfloat16))
    normed_grad = jnp.dot(pre_grad, w_in.T, preferred_element_type=jnp.float32).astype(jnp.bfloat16)
    scaled_grad = normed_grad.astype(jnp.float32).reshape(grad.shape) * norm_gain
    inner = jnp.sum(scaled_grad * modulated, axis=-1, keepdims=True)
    modulated_grad = inv_rms * scaled_grad - modulated * (inv_rms * inv_rms * inv_rms) * (inner / channels)
    stencil_grad = modulated_grad * (1.0 + modulate[:, 0])[:, None, None, :]
    spread = stencil(
        stencil_grad.reshape(clip_count, frame_count, H, W, channels), stencil_taps[::-1]
    ).reshape(grad.shape)
    return (grad.astype(jnp.float32) + spread.astype(jnp.bfloat16).astype(jnp.float32)).astype(jnp.bfloat16)


def band_frames(values, tap_table):
    frame_count = values.shape[1]
    reach = BAND // 2
    volume = values.astype(jnp.float32)
    padded = jnp.pad(volume, ((0, 0), (reach, reach), (0, 0), (0, 0)))
    total = volume
    for offset in range(BAND):
        total = total + tap_table[:, offset, None, None, :] * padded[:, offset : offset + frame_count]
    return total.astype(jnp.bfloat16)


def temporal(values, tap_table):
    clip_count, frame_count, pixel_count, channels = values.shape
    groups = lax.axis_size("seq")
    grouped = values.reshape(clip_count, frame_count, groups, pixel_count // groups, channels)
    pixel_view = lax.all_to_all(grouped, "seq", split_axis=2, concat_axis=1, tiled=True)
    pixel_view = pixel_view.reshape(clip_count, groups * frame_count, pixel_count // groups, channels)
    banded = band_frames(pixel_view, tap_table)
    banded = banded.reshape(clip_count, groups * frame_count, 1, pixel_count // groups, channels)
    back = lax.all_to_all(banded, "seq", split_axis=1, concat_axis=2, tiled=True)
    return back.reshape(values.shape)


def temporal_shared(values, tap_table):
    clip_count, frame_count, pixel_count, channels = values.shape
    groups = lax.axis_size("seq")
    planes = lax.axis_size("section")
    grouped = values.reshape(clip_count, frame_count, groups, pixel_count // groups, channels)
    pixel_view = lax.all_to_all(grouped, "seq", split_axis=2, concat_axis=1, tiled=True)
    pixel_view = pixel_view.reshape(clip_count, groups * frame_count, pixel_count // groups, channels)
    banded = band_frames(pixel_view, tap_table)
    banded = jnp.broadcast_to(
        banded[:, None], (clip_count, planes) + banded.shape[1:]
    ).reshape(clip_count, planes * groups * frame_count, 1, pixel_count // groups, channels)
    back = lax.all_to_all(banded, ("section", "seq"), split_axis=1, concat_axis=2, tiled=True)
    back = back.reshape(clip_count, frame_count, planes, pixel_count, channels)
    return jnp.moveaxis(back, 2, 0)


def on_device(clips, cotangent, spatial_taps, modulation, norm_gain, w_in, w_out, band_taps):
    first = lax.axis_index("section") == 0
    taps, mod, gain = spatial_taps[0], modulation[0], norm_gain[0]
    weight_in, weight_out, band = w_in[0], w_out[0], band_taps[0]

    to_first = [(1, 0)]
    core = lax.axis_index("seq") % 2
    siblings = [(q, q ^ 1) for q in range(lax.axis_size("seq"))]

    def fetch_halves(p):
        half = p.shape[0] // 2
        mine = lax.dynamic_slice_in_dim(p, core * half, half, 0)
        got = lax.ppermute(mine, "section", perm=to_first)
        other = lax.ppermute(got, "seq", perm=siblings)
        return jnp.where(core == 0, jnp.concatenate([got, other]), jnp.concatenate([other, got]))

    second_taps, second_mod, second_gain = [
        jnp.where(first, lax.ppermute(p, "section", perm=to_first), p)
        for p in (taps, mod, gain)
    ]
    second_in, second_out = lax.optimization_barrier(
        [jnp.where(first, fetch_halves(p), p) for p in (weight_in, weight_out)]
    )

    first_params = (taps, mod, gain, weight_in, weight_out)
    second_params = (second_taps, second_mod, second_gain, second_in, second_out)

    first_mixed, first_saved = spatial_forward(clips, *first_params)
    lead_in = jnp.where(first, first_mixed, cotangent)
    lead_taps = jnp.where(first, band, band[::-1])
    first_acts, second_seed = temporal_shared(lead_in, lead_taps[None])
    second_mixed, second_saved = spatial_forward(first_acts, *second_params)
    second_grad = spatial_backward(second_saved, second_seed, *second_params)

    tail_in = jnp.where(first, second_grad, second_mixed)
    tail_taps = jnp.where(first, band[::-1], band)
    tail_out = temporal(tail_in, tail_taps[None])
    first_grad = spatial_backward(first_saved, tail_out, *first_params)

    activations = jnp.where(first, first_acts, tail_out)
    input_grads = jnp.where(first, first_grad, second_grad)
    return (activations[None], input_grads[None])


def solution(mesh):
    placed = (
        P(None, "seq", None, None),
        P(None, "seq", None, None),
        P("section", None, None),
        P("section", None, None, None),
        P("section", None),
        P("section", None, None),
        P("section", None, None),
        P("section", None, None),
    )
    return jax.shard_map(
        on_device,
        mesh=mesh,
        in_specs=placed,
        out_specs=(P("section", None, "seq", None, None), P("section", None, "seq", None, None)),
        check_vma=False,
    )
```

```python
import jax
import jax.numpy as jnp
from jax import lax
from jax.sharding import PartitionSpec as P

H = 32
W = 16
BAND = 9


EPSILON = 1e-06


def stencil(volume, stencil_taps):
    padded = jnp.pad(volume, ((0, 0), (0, 0), (1, 1), (1, 1), (0, 0)))
    total = jnp.zeros_like(volume)
    for down_step in range(3):
        for across in range(3):
            total = total + stencil_taps[3 * down_step + across] * padded[
                :, :, down_step : down_step + H, across : across + W
            ]
    return total


def spatial_forward(values, stencil_taps, modulate, norm_gain, w_in, w_out):
    clip_count, frame_count, pixel_count, channels = values.shape
    volume = values.astype(jnp.float32).reshape(clip_count, frame_count, H, W, channels)
    stencil_sum = stencil(volume, stencil_taps).reshape(values.shape)
    scale = (1.0 + modulate[:, 0])[:, None, None, :]
    shift = modulate[:, 1][:, None, None, :]
    modulated = stencil_sum * scale + shift
    inv_rms = lax.rsqrt(jnp.mean(modulated * modulated, axis=-1, keepdims=True) + EPSILON)
    normed = (modulated * inv_rms * norm_gain).astype(jnp.bfloat16).reshape(-1, channels)
    pre = jnp.dot(normed, w_in, preferred_element_type=jnp.float32)
    hidden = jax.nn.silu(pre).astype(jnp.bfloat16)
    update = jnp.dot(hidden, w_out, preferred_element_type=jnp.float32)
    out = (values.astype(jnp.float32) + update.reshape(values.shape)).astype(jnp.bfloat16)
    return out, (modulated, inv_rms, pre)


def spatial_backward(saved, grad, stencil_taps, modulate, norm_gain, w_in, w_out):
    modulated, inv_rms, pre = saved
    clip_count, frame_count, pixel_count, channels = grad.shape
    flat_grad = grad.reshape(-1, channels)
    hidden_grad = jnp.dot(flat_grad, w_out.T, preferred_element_type=jnp.float32).astype(jnp.bfloat16)
    gate = jax.nn.sigmoid(pre)
    pre_grad = hidden_grad.astype(jnp.float32) * (gate * (1.0 + pre * (1.0 - gate)))
    pre_grad = lax.optimization_barrier(pre_grad.astype(jnp.bfloat16))
    normed_grad = jnp.dot(pre_grad, w_in.T, preferred_element_type=jnp.float32).astype(jnp.bfloat16)
    scaled_grad = normed_grad.astype(jnp.float32).reshape(grad.shape) * norm_gain
    inner = jnp.sum(scaled_grad * modulated, axis=-1, keepdims=True)
    modulated_grad = inv_rms * scaled_grad - modulated * (inv_rms * inv_rms * inv_rms) * (inner / channels)
    stencil_grad = modulated_grad * (1.0 + modulate[:, 0])[:, None, None, :]
    spread = stencil(
        stencil_grad.reshape(clip_count, frame_count, H, W, channels), stencil_taps[::-1]
    ).reshape(grad.shape)
    return (grad.astype(jnp.float32) + spread.astype(jnp.bfloat16).astype(jnp.float32)).astype(jnp.bfloat16)


def band_frames(values, tap_table):
    frame_count = values.shape[1]
    reach = BAND // 2
    volume = values.astype(jnp.float32)
    padded = jnp.pad(volume, ((0, 0), (reach, reach), (0, 0), (0, 0)))
    total = volume
    for offset in range(BAND):
        total = total + tap_table[:, offset, None, None, :] * padded[:, offset : offset + frame_count]
    return total.astype(jnp.bfloat16)


def temporal(values, tap_table, carried):
    clip_count, frame_count, pixel_count, channels = values.shape
    groups = lax.axis_size("seq")
    grouped = values.reshape(clip_count, frame_count, groups, pixel_count // groups, channels)
    pixel_view = lax.all_to_all(grouped, "seq", split_axis=2, concat_axis=1, tiled=True)
    pixel_view, carried = lax.optimization_barrier((pixel_view, carried))
    pixel_view = pixel_view.reshape(clip_count, groups * frame_count, pixel_count // groups, channels)
    banded = band_frames(pixel_view, tap_table)
    banded = banded.reshape(clip_count, groups * frame_count, 1, pixel_count // groups, channels)
    back = lax.all_to_all(banded, "seq", split_axis=1, concat_axis=2, tiled=True)
    return back.reshape(values.shape), carried


def on_device(clips, cotangent, spatial_taps, modulation, norm_gain, w_in, w_out, band_taps):
    first = lax.axis_index("section") == 0
    taps, mod, gain = spatial_taps[0], modulation[0], norm_gain[0]
    weight_in, weight_out, band = w_in[0], w_out[0], band_taps[0]
    channels = taps.shape[-1]
    first_params = (taps, mod, gain, weight_in, weight_out)

    first_mixed, first_saved = spatial_forward(clips, *first_params)
    lead_in = jnp.where(first, first_mixed, cotangent)
    lead_taps = jnp.where(first, band, band[::-1])

    lead_in, fetched = lax.optimization_barrier((lead_in, first_params))
    to_first = [(1, 0)]
    core = lax.axis_index("seq") % 2
    siblings = [(q, q ^ 1) for q in range(lax.axis_size("seq"))]
    f_taps, f_mod, f_gain, f_in, f_out = fetched
    small = jnp.concatenate([f_taps, f_mod.reshape(-1, channels), f_gain[None]])
    got_small = lax.ppermute(small, "section", perm=to_first)
    in_half, out_half = f_in.shape[0] // 2, f_out.shape[0] // 2
    halves = jnp.concatenate(
        [
            lax.dynamic_slice_in_dim(f_in, core * in_half, in_half, 0).reshape(-1),
            lax.dynamic_slice_in_dim(f_out, core * out_half, out_half, 0).reshape(-1),
        ]
    )
    got = lax.ppermute(halves, "section", perm=to_first)
    other = lax.ppermute(got, "seq", perm=siblings)
    low, high = jnp.where(core == 0, got, other), jnp.where(core == 0, other, got)
    split = in_half * f_in.shape[1]
    got_in = jnp.concatenate([low[:split], high[:split]]).reshape(f_in.shape)
    got_out = jnp.concatenate([low[split:], high[split:]]).reshape(f_out.shape)
    tap_count = f_taps.shape[0]
    got_taps = got_small[:tap_count]
    got_mod = got_small[tap_count:-1].reshape(f_mod.shape)
    got_gain = got_small[-1]
    second_params = tuple(
        jnp.where(first, g, p)
        for g, p in zip((got_taps, got_mod, got_gain, got_in, got_out), first_params)
    )

    lead_out, second_params = temporal(lead_in, lead_taps[None], second_params)

    swapped = lax.ppermute(lead_out, "section", perm=[(0, 1), (1, 0)])
    first_acts = jnp.where(first, lead_out, swapped)
    second_seed = jnp.where(first, swapped, lead_out)
    second_mixed, second_saved = spatial_forward(first_acts, *second_params)
    second_grad = spatial_backward(second_saved, second_seed, *second_params)

    tail_in = jnp.where(first, second_grad, second_mixed)
    tail_taps = jnp.where(first, band[::-1], band)
    tail_out, _ = temporal(tail_in, tail_taps[None], ())
    first_grad = spatial_backward(first_saved, tail_out, *first_params)

    activations = jnp.where(first, lead_out, tail_out)
    input_grads = jnp.where(first, first_grad, second_grad)
    return (activations[None], input_grads[None])


def solution(mesh):
    placed = (
        P(None, "seq", None, None),
        P(None, "seq", None, None),
        P("section", None, None),
        P("section", None, None, None),
        P("section", None),
        P("section", None, None),
        P("section", None, None),
        P("section", None, None),
    )
    return jax.shard_map(
        on_device,
        mesh=mesh,
        in_specs=placed,
        out_specs=(P("section", None, "seq", None, None), P("section", None, "seq", None, None)),
        check_vma=False,
    )
```

```python
import jax
import jax.numpy as jnp
from jax import lax
from jax.sharding import PartitionSpec as P

H = 32
W = 16
BAND = 9


EPSILON = 1e-06


def stencil(volume, stencil_taps):
    channels = volume.shape[-1]
    kernel = stencil_taps.reshape(3, 3, 1, channels)
    total = lax.conv_general_dilated(
        volume.reshape(-1, H, W, channels),
        kernel,
        window_strides=(1, 1),
        padding=((1, 1), (1, 1)),
        dimension_numbers=("NHWC", "HWIO", "NHWC"),
        feature_group_count=channels,
        precision=lax.Precision.HIGHEST,
    )
    return total.reshape(volume.shape)


def spatial_forward(values, stencil_taps, modulate, norm_gain, w_in, w_out):
    clip_count, frame_count, pixel_count, channels = values.shape
    volume = values.astype(jnp.float32).reshape(clip_count, frame_count, H, W, channels)
    stencil_sum = stencil(volume, stencil_taps).reshape(values.shape)
    scale = (1.0 + modulate[:, 0])[:, None, None, :]
    shift = modulate[:, 1][:, None, None, :]
    modulated = stencil_sum * scale + shift
    inv_rms = lax.rsqrt(jnp.mean(modulated * modulated, axis=-1, keepdims=True) + EPSILON)
    normed = (modulated * inv_rms * norm_gain).astype(jnp.bfloat16).reshape(-1, channels)
    pre = jnp.dot(normed, w_in, preferred_element_type=jnp.float32)
    hidden = jax.nn.silu(pre).astype(jnp.bfloat16)
    update = jnp.dot(hidden, w_out, preferred_element_type=jnp.float32)
    out = (values.astype(jnp.float32) + update.reshape(values.shape)).astype(jnp.bfloat16)
    return out, (modulated, inv_rms, pre)


def spatial_backward(saved, grad, stencil_taps, modulate, norm_gain, w_in, w_out):
    modulated, inv_rms, pre = saved
    clip_count, frame_count, pixel_count, channels = grad.shape
    flat_grad = grad.reshape(-1, channels)
    hidden_grad = jnp.dot(flat_grad, w_out.T, preferred_element_type=jnp.float32).astype(jnp.bfloat16)
    gate = jax.nn.sigmoid(pre)
    pre_grad = hidden_grad.astype(jnp.float32) * (gate * (1.0 + pre * (1.0 - gate)))
    pre_grad = lax.optimization_barrier(pre_grad.astype(jnp.bfloat16))
    normed_grad = jnp.dot(pre_grad, w_in.T, preferred_element_type=jnp.float32).astype(jnp.bfloat16)
    scaled_grad = normed_grad.astype(jnp.float32).reshape(grad.shape) * norm_gain
    inner = jnp.sum(scaled_grad * modulated, axis=-1, keepdims=True)
    modulated_grad = inv_rms * scaled_grad - modulated * (inv_rms * inv_rms * inv_rms) * (inner / channels)
    stencil_grad = modulated_grad * (1.0 + modulate[:, 0])[:, None, None, :]
    spread = stencil(
        stencil_grad.reshape(clip_count, frame_count, H, W, channels), stencil_taps[::-1]
    ).reshape(grad.shape)
    return (grad.astype(jnp.float32) + spread.astype(jnp.bfloat16).astype(jnp.float32)).astype(jnp.bfloat16)


def band_frames(values, tap_table):
    frame_count = values.shape[1]
    reach = BAND // 2
    volume = values.astype(jnp.float32)
    padded = jnp.pad(volume, ((0, 0), (reach, reach), (0, 0), (0, 0)))
    total = volume
    for offset in range(BAND):
        total = total + tap_table[:, offset, None, None, :] * padded[:, offset : offset + frame_count]
    return total.astype(jnp.bfloat16)


def temporal(values, tap_table):
    clip_count, frame_count, pixel_count, channels = values.shape
    groups = lax.axis_size("seq")
    grouped = values.reshape(clip_count, frame_count, groups, pixel_count // groups, channels)
    pixel_view = lax.all_to_all(grouped, "seq", split_axis=2, concat_axis=1, tiled=True)
    pixel_view = pixel_view.reshape(clip_count, groups * frame_count, pixel_count // groups, channels)
    banded = band_frames(pixel_view, tap_table)
    banded = banded.reshape(clip_count, groups * frame_count, 1, pixel_count // groups, channels)
    back = lax.all_to_all(banded, "seq", split_axis=1, concat_axis=2, tiled=True)
    return back.reshape(values.shape)


def temporal_shared(values, tap_table):
    clip_count, frame_count, pixel_count, channels = values.shape
    groups = lax.axis_size("seq")
    planes = lax.axis_size("section")
    grouped = values.reshape(clip_count, frame_count, groups, pixel_count // groups, channels)
    pixel_view = lax.all_to_all(grouped, "seq", split_axis=2, concat_axis=1, tiled=True)
    pixel_view = pixel_view.reshape(clip_count, groups * frame_count, pixel_count // groups, channels)
    banded = band_frames(pixel_view, tap_table)
    banded = jnp.broadcast_to(
        banded[:, None], (clip_count, planes) + banded.shape[1:]
    ).reshape(clip_count, planes * groups * frame_count, 1, pixel_count // groups, channels)
    back = lax.all_to_all(banded, ("section", "seq"), split_axis=1, concat_axis=2, tiled=True)
    back = back.reshape(clip_count, frame_count, planes, pixel_count, channels)
    return jnp.moveaxis(back, 2, 0)


def on_device(clips, cotangent, spatial_taps, modulation, norm_gain, w_in, w_out, band_taps):
    first = lax.axis_index("section") == 0
    taps, mod, gain = spatial_taps[0], modulation[0], norm_gain[0]
    weight_in, weight_out, band = w_in[0], w_out[0], band_taps[0]

    to_first = [(1, 0)]
    core = lax.axis_index("seq") % 2
    siblings = [(q, q ^ 1) for q in range(lax.axis_size("seq"))]

    def fetch_halves(p):
        half = p.shape[0] // 2
        mine = lax.dynamic_slice_in_dim(p, core * half, half, 0)
        got = lax.ppermute(mine, "section", perm=to_first)
        other = lax.ppermute(got, "seq", perm=siblings)
        return jnp.where(core == 0, jnp.concatenate([got, other]), jnp.concatenate([other, got]))

    second_taps, second_mod, second_gain = [
        jnp.where(first, lax.ppermute(p, "section", perm=to_first), p)
        for p in (taps, mod, gain)
    ]
    second_in, second_out = lax.optimization_barrier(
        [jnp.where(first, fetch_halves(p), p) for p in (weight_in, weight_out)]
    )

    first_params = (taps, mod, gain, weight_in, weight_out)
    second_params = (second_taps, second_mod, second_gain, second_in, second_out)

    first_mixed, first_saved = spatial_forward(clips, *first_params)
    lead_in = jnp.where(first, first_mixed, cotangent)
    lead_taps = jnp.where(first, band, band[::-1])
    first_acts, second_seed = temporal_shared(lead_in, lead_taps[None])
    second_mixed, second_saved = spatial_forward(first_acts, *second_params)
    second_grad = spatial_backward(second_saved, second_seed, *second_params)

    tail_in = jnp.where(first, second_grad, second_mixed)
    tail_taps = jnp.where(first, band[::-1], band)
    tail_out = temporal(tail_in, tail_taps[None])
    first_grad = spatial_backward(first_saved, tail_out, *first_params)

    activations = jnp.where(first, first_acts, tail_out)
    input_grads = jnp.where(first, first_grad, second_grad)
    return (activations[None], input_grads[None])


def solution(mesh):
    placed = (
        P(None, "seq", None, None),
        P(None, "seq", None, None),
        P("section", None, None),
        P("section", None, None, None),
        P("section", None),
        P("section", None, None),
        P("section", None, None),
        P("section", None, None),
    )
    return jax.shard_map(
        on_device,
        mesh=mesh,
        in_specs=placed,
        out_specs=(P("section", None, "seq", None, None), P("section", None, "seq", None, None)),
        check_vma=False,
    )
```

```python
import jax
import jax.numpy as jnp
from jax import lax
from jax.sharding import PartitionSpec as P

H = 32
W = 16
BAND = 9


EPSILON = 1e-06


def stencil(volume, stencil_taps):
    padded = jnp.pad(volume, ((0, 0), (0, 0), (1, 1), (1, 1), (0, 0)))
    total = jnp.zeros_like(volume)
    for down_step in range(3):
        for across in range(3):
            total = total + stencil_taps[3 * down_step + across] * padded[
                :, :, down_step : down_step + H, across : across + W
            ]
    return total


def spatial_forward(values, stencil_taps, modulate, norm_gain, w_in, w_out):
    clip_count, frame_count, pixel_count, channels = values.shape
    volume = values.astype(jnp.float32).reshape(clip_count, frame_count, H, W, channels)
    stencil_sum = stencil(volume, stencil_taps).reshape(values.shape)
    scale = (1.0 + modulate[:, 0])[:, None, None, :]
    shift = modulate[:, 1][:, None, None, :]
    modulated = stencil_sum * scale + shift
    inv_rms = lax.rsqrt(jnp.mean(modulated * modulated, axis=-1, keepdims=True) + EPSILON)
    normed = (modulated * inv_rms * norm_gain).astype(jnp.bfloat16).reshape(-1, channels)
    pre = jnp.dot(normed, w_in, preferred_element_type=jnp.float32)
    hidden = jax.nn.silu(pre).astype(jnp.bfloat16)
    update = jnp.dot(hidden, w_out, preferred_element_type=jnp.float32)
    out = (values.astype(jnp.float32) + update.reshape(values.shape)).astype(jnp.bfloat16)
    return out, (modulated, inv_rms, pre)


def spatial_backward(saved, grad, stencil_taps, modulate, norm_gain, w_in, w_out):
    modulated, inv_rms, pre = saved
    clip_count, frame_count, pixel_count, channels = grad.shape
    flat_grad = grad.reshape(-1, channels)
    hidden_grad = jnp.dot(flat_grad, w_out.T, preferred_element_type=jnp.float32).astype(jnp.bfloat16)
    gate = jax.nn.sigmoid(pre)
    pre_grad = hidden_grad.astype(jnp.float32) * (gate * (1.0 + pre * (1.0 - gate)))
    pre_grad = lax.optimization_barrier(pre_grad.astype(jnp.bfloat16))
    normed_grad = jnp.dot(pre_grad, w_in.T, preferred_element_type=jnp.float32).astype(jnp.bfloat16)
    scaled_grad = normed_grad.astype(jnp.float32).reshape(grad.shape) * norm_gain
    inner = jnp.sum(scaled_grad * modulated, axis=-1, keepdims=True)
    modulated_grad = inv_rms * scaled_grad - modulated * (inv_rms * inv_rms * inv_rms) * (inner / channels)
    stencil_grad = modulated_grad * (1.0 + modulate[:, 0])[:, None, None, :]
    spread = stencil(
        stencil_grad.reshape(clip_count, frame_count, H, W, channels), stencil_taps[::-1]
    ).reshape(grad.shape)
    return (grad.astype(jnp.float32) + spread.astype(jnp.bfloat16).astype(jnp.float32)).astype(jnp.bfloat16)


def band_frames(values, tap_table):
    frame_count = values.shape[1]
    reach = BAND // 2
    volume = values.astype(jnp.float32)
    padded = jnp.pad(volume, ((0, 0), (reach, reach), (0, 0), (0, 0)))
    total = volume
    for offset in range(BAND):
        total = total + tap_table[:, offset, None, None, :] * padded[:, offset : offset + frame_count]
    return total.astype(jnp.bfloat16)


def temporal(values, tap_table):
    clip_count, frame_count, pixel_count, channels = values.shape
    groups = lax.axis_size("seq")
    grouped = values.reshape(clip_count, frame_count, groups, pixel_count // groups, channels)
    pixel_view = lax.all_to_all(grouped, "seq", split_axis=2, concat_axis=1, tiled=True)
    pixel_view = pixel_view.reshape(clip_count, groups * frame_count, pixel_count // groups, channels)
    banded = band_frames(pixel_view, tap_table)
    banded = banded.reshape(clip_count, groups * frame_count, 1, pixel_count // groups, channels)
    back = lax.all_to_all(banded, "seq", split_axis=1, concat_axis=2, tiled=True)
    return back.reshape(values.shape)


def on_device(clips, cotangent, spatial_taps, modulation, norm_gain, w_in, w_out, band_taps):
    first = lax.axis_index("section") == 0
    taps, mod, gain = spatial_taps[0], modulation[0], norm_gain[0]
    weight_in, weight_out, band = w_in[0], w_out[0], band_taps[0]

    to_first = [(1, 0)]
    core = lax.axis_index("seq") % 2
    siblings = [(q, q ^ 1) for q in range(lax.axis_size("seq"))]

    def fetch_halves(p):
        half = p.shape[0] // 2
        mine = lax.dynamic_slice_in_dim(p, core * half, half, 0)
        got = lax.ppermute(mine, "section", perm=to_first)
        other = lax.ppermute(got, "seq", perm=siblings)
        return jnp.where(core == 0, jnp.concatenate([got, other]), jnp.concatenate([other, got]))

    second_taps, second_mod, second_gain = [
        jnp.where(first, lax.ppermute(p, "section", perm=to_first), p)
        for p in (taps, mod, gain)
    ]
    second_in, second_out = lax.optimization_barrier(
        [jnp.where(first, fetch_halves(p), p) for p in (weight_in, weight_out)]
    )

    first_params = (taps, mod, gain, weight_in, weight_out)
    second_params = (second_taps, second_mod, second_gain, second_in, second_out)

    first_mixed, first_saved = spatial_forward(clips, *first_params)
    lead_in = jnp.where(first, first_mixed, cotangent)
    lead_taps = jnp.where(first, band, band[::-1])
    lead_out = temporal(lead_in, lead_taps[None])

    second_seed = lax.ppermute(lead_out, "section", perm=to_first)
    second_mixed, second_saved = spatial_forward(lead_out, *second_params)
    second_grad = spatial_backward(second_saved, second_seed, *second_params)

    to_second = [(0, 1)]
    sent_mixed = lax.ppermute(second_mixed, "section", perm=to_second)
    sent_grad = lax.ppermute(second_grad, "section", perm=to_second)
    tail_in = jnp.where(first, second_grad, sent_mixed)
    tail_taps = jnp.where(first, band[::-1], band)
    tail_out = temporal(tail_in, tail_taps[None])
    first_grad = spatial_backward(first_saved, tail_out, *first_params)

    activations = jnp.where(first, lead_out, tail_out)
    input_grads = jnp.where(first, first_grad, sent_grad)
    return (activations[None], input_grads[None])


def solution(mesh):
    placed = (
        P(None, "seq", None, None),
        P(None, "seq", None, None),
        P("section", None, None),
        P("section", None, None, None),
        P("section", None),
        P("section", None, None),
        P("section", None, None),
        P("section", None, None),
    )
    return jax.shard_map(
        on_device,
        mesh=mesh,
        in_specs=placed,
        out_specs=(P("section", None, "seq", None, None), P("section", None, "seq", None, None)),
        check_vma=False,
    )
```

```python
import jax
import jax.numpy as jnp
from jax import lax
from jax.sharding import PartitionSpec as P

H = 32
W = 16
BAND = 9


EPSILON = 1e-06


def stencil(volume, stencil_taps):
    padded = jnp.pad(volume, ((0, 0), (0, 0), (1, 1), (1, 1), (0, 0)))
    total = jnp.zeros_like(volume)
    for down_step in range(3):
        for across in range(3):
            total = total + stencil_taps[3 * down_step + across] * padded[
                :, :, down_step : down_step + H, across : across + W
            ]
    return total


def spatial_forward(values, stencil_taps, modulate, norm_gain, w_in, w_out):
    clip_count, frame_count, pixel_count, channels = values.shape
    volume = values.astype(jnp.float32).reshape(clip_count, frame_count, H, W, channels)
    stencil_sum = stencil(volume, stencil_taps).reshape(values.shape)
    scale = (1.0 + modulate[:, 0])[:, None, None, :]
    shift = modulate[:, 1][:, None, None, :]
    modulated = stencil_sum * scale + shift
    inv_rms = lax.rsqrt(jnp.mean(modulated * modulated, axis=-1, keepdims=True) + EPSILON)
    normed = (modulated * inv_rms * norm_gain).astype(jnp.bfloat16).reshape(-1, channels)
    pre = jnp.dot(normed, w_in, preferred_element_type=jnp.float32)
    hidden = jax.nn.silu(pre).astype(jnp.bfloat16)
    update = jnp.dot(hidden, w_out, preferred_element_type=jnp.float32)
    out = (values.astype(jnp.float32) + update.reshape(values.shape)).astype(jnp.bfloat16)
    return out, (modulated, inv_rms, pre)


def spatial_backward(saved, grad, stencil_taps, modulate, norm_gain, w_in, w_out):
    modulated, inv_rms, pre = saved
    clip_count, frame_count, pixel_count, channels = grad.shape
    flat_grad = grad.reshape(-1, channels)
    hidden_grad = jnp.dot(flat_grad, w_out.T, preferred_element_type=jnp.float32).astype(jnp.bfloat16)
    gate = jax.nn.sigmoid(pre)
    pre_grad = hidden_grad.astype(jnp.float32) * (gate * (1.0 + pre * (1.0 - gate)))
    pre_grad = lax.optimization_barrier(pre_grad.astype(jnp.bfloat16))
    normed_grad = jnp.dot(pre_grad, w_in.T, preferred_element_type=jnp.float32).astype(jnp.bfloat16)
    scaled_grad = normed_grad.astype(jnp.float32).reshape(grad.shape) * norm_gain
    inner = jnp.sum(scaled_grad * modulated, axis=-1, keepdims=True)
    modulated_grad = inv_rms * scaled_grad - modulated * (inv_rms * inv_rms * inv_rms) * (inner / channels)
    stencil_grad = modulated_grad * (1.0 + modulate[:, 0])[:, None, None, :]
    spread = stencil(
        stencil_grad.reshape(clip_count, frame_count, H, W, channels), stencil_taps[::-1]
    ).reshape(grad.shape)
    return (grad.astype(jnp.float32) + spread.astype(jnp.bfloat16).astype(jnp.float32)).astype(jnp.bfloat16)


def band_frames(values, tap_table):
    frame_count = values.shape[1]
    reach = BAND // 2
    volume = values.astype(jnp.float32)
    padded = jnp.pad(volume, ((0, 0), (reach, reach), (0, 0), (0, 0)))
    total = volume
    for offset in range(BAND):
        total = total + tap_table[:, offset, None, None, :] * padded[:, offset : offset + frame_count]
    return total.astype(jnp.bfloat16)


def temporal(values, tap_table):
    clip_count, frame_count, pixel_count, channels = values.shape
    groups = lax.axis_size("seq")
    grouped = values.reshape(clip_count, frame_count, groups, pixel_count // groups, channels)
    pixel_view = lax.all_to_all(grouped, "seq", split_axis=2, concat_axis=1, tiled=True)
    pixel_view = pixel_view.reshape(clip_count, groups * frame_count, pixel_count // groups, channels)
    banded = band_frames(pixel_view, tap_table)
    banded = banded.reshape(clip_count, groups * frame_count, 1, pixel_count // groups, channels)
    back = lax.all_to_all(banded, "seq", split_axis=1, concat_axis=2, tiled=True)
    return back.reshape(values.shape)


def on_device(clips, cotangent, spatial_taps, modulation, norm_gain, w_in, w_out, band_taps):
    first = lax.axis_index("section") == 0
    taps, mod, gain = spatial_taps[0], modulation[0], norm_gain[0]
    weight_in, weight_out, band = w_in[0], w_out[0], band_taps[0]
    clip_total = clips.shape[0]

    to_first = [(1, 0)]
    core = lax.axis_index("seq") % 2
    siblings = [(q, q ^ 1) for q in range(lax.axis_size("seq"))]

    def fetch_halves(p):
        half = p.shape[0] // 2
        mine = lax.dynamic_slice_in_dim(p, core * half, half, 0)
        got = lax.ppermute(mine, "section", perm=to_first)
        other = lax.ppermute(got, "seq", perm=siblings)
        return jnp.where(core == 0, jnp.concatenate([got, other]), jnp.concatenate([other, got]))

    second_taps, second_mod, second_gain = [
        jnp.where(first, lax.ppermute(p, "section", perm=to_first), p)
        for p in (taps, mod, gain)
    ]
    second_in, second_out = lax.optimization_barrier(
        [jnp.where(first, fetch_halves(p), p) for p in (weight_in, weight_out)]
    )

    first_params = (taps, mod, gain, weight_in, weight_out)
    second_params = (second_taps, second_mod, second_gain, second_in, second_out)

    first_mixed, first_saved = spatial_forward(clips, *first_params)
    lead_in = jnp.where(first, first_mixed, cotangent)
    lead_taps = jnp.where(first, band, band[::-1])
    lead_out = temporal(lead_in, lead_taps[None])

    second_mixed, second_saved = spatial_forward(lead_out, *second_params)
    rows = second_saved[2].shape[0] // clip_total
    second_grad = []
    outgoing = lead_out[:1]
    for clip in range(clip_total):
        second_seed = lax.ppermute(outgoing, "section", perm=to_first)
        if clip + 1 < clip_total:
            second_seed, outgoing = lax.optimization_barrier(
                (second_seed, lead_out[clip + 1 : clip + 2])
            )
        saved = (
            second_saved[0][clip : clip + 1],
            second_saved[1][clip : clip + 1],
            second_saved[2][clip * rows : (clip + 1) * rows],
        )
        clip_params = list(second_params)
        clip_params[1] = second_params[1][clip : clip + 1]
        second_grad.append(spatial_backward(saved, second_seed, *clip_params))
    second_grad = jnp.concatenate(second_grad)

    to_second = [(0, 1)]
    sent_mixed = lax.ppermute(second_mixed, "section", perm=to_second)
    sent_grad = lax.ppermute(second_grad, "section", perm=to_second)
    tail_in = jnp.where(first, second_grad, sent_mixed)
    tail_taps = jnp.where(first, band[::-1], band)
    tail_out = temporal(tail_in, tail_taps[None])
    first_grad = spatial_backward(first_saved, tail_out, *first_params)

    activations = jnp.where(first, lead_out, tail_out)
    input_grads = jnp.where(first, first_grad, sent_grad)
    return (activations[None], input_grads[None])


def solution(mesh):
    placed = (
        P(None, "seq", None, None),
        P(None, "seq", None, None),
        P("section", None, None),
        P("section", None, None, None),
        P("section", None),
        P("section", None, None),
        P("section", None, None),
        P("section", None, None),
    )
    return jax.shard_map(
        on_device,
        mesh=mesh,
        in_specs=placed,
        out_specs=(P("section", None, "seq", None, None), P("section", None, "seq", None, None)),
        check_vma=False,
    )
```

```python
import jax
import jax.numpy as jnp
from jax import lax
from jax.sharding import PartitionSpec as P

H = 32
W = 16
BAND = 9


EPSILON = 1e-06


def stencil(volume, stencil_taps):
    zero = ((0, 0), (0, 0))
    padded = jnp.pad(volume, zero + ((1, 1), (0, 0), (0, 0)))
    columns = []
    for across in range(3):
        column = stencil_taps[across] * padded[:, :, 0:H]
        for down_step in range(1, 3):
            column = column + stencil_taps[3 * down_step + across] * padded[:, :, down_step : down_step + H]
        columns.append(column)
    left = jnp.pad(columns[0], zero + ((0, 0), (1, 0), (0, 0)))[:, :, :, :W]
    right = jnp.pad(columns[2], zero + ((0, 0), (0, 1), (0, 0)))[:, :, :, 1:]
    return left + columns[1] + right


def spatial_forward(values, stencil_taps, modulate, norm_gain, w_in, w_out):
    clip_count, frame_count, pixel_count, channels = values.shape
    volume = values.astype(jnp.float32).reshape(clip_count, frame_count, H, W, channels)
    stencil_sum = stencil(volume, stencil_taps).reshape(values.shape)
    scale = (1.0 + modulate[:, 0])[:, None, None, :]
    shift = modulate[:, 1][:, None, None, :]
    modulated = stencil_sum * scale + shift
    inv_rms = lax.rsqrt(jnp.mean(modulated * modulated, axis=-1, keepdims=True) + EPSILON)
    normed = (modulated * inv_rms * norm_gain).astype(jnp.bfloat16).reshape(-1, channels)
    pre = jnp.dot(normed, w_in, preferred_element_type=jnp.float32)
    hidden = jax.nn.silu(pre).astype(jnp.bfloat16)
    update = jnp.dot(hidden, w_out, preferred_element_type=jnp.float32)
    out = (values.astype(jnp.float32) + update.reshape(values.shape)).astype(jnp.bfloat16)
    return out, (modulated, inv_rms, pre)


def spatial_backward(saved, grad, stencil_taps, modulate, norm_gain, w_in, w_out):
    modulated, inv_rms, pre = saved
    clip_count, frame_count, pixel_count, channels = grad.shape
    flat_grad = grad.reshape(-1, channels)
    hidden_grad = jnp.dot(flat_grad, w_out.T, preferred_element_type=jnp.float32).astype(jnp.bfloat16)
    gate = jax.nn.sigmoid(pre)
    pre_grad = hidden_grad.astype(jnp.float32) * (gate * (1.0 + pre * (1.0 - gate)))
    pre_grad = lax.optimization_barrier(pre_grad.astype(jnp.bfloat16))
    normed_grad = jnp.dot(pre_grad, w_in.T, preferred_element_type=jnp.float32).astype(jnp.bfloat16)
    scaled_grad = normed_grad.astype(jnp.float32).reshape(grad.shape) * norm_gain
    inner = jnp.sum(scaled_grad * modulated, axis=-1, keepdims=True)
    modulated_grad = inv_rms * scaled_grad - modulated * (inv_rms * inv_rms * inv_rms) * (inner / channels)
    stencil_grad = modulated_grad * (1.0 + modulate[:, 0])[:, None, None, :]
    spread = stencil(
        stencil_grad.reshape(clip_count, frame_count, H, W, channels), stencil_taps[::-1]
    ).reshape(grad.shape)
    return (grad.astype(jnp.float32) + spread.astype(jnp.bfloat16).astype(jnp.float32)).astype(jnp.bfloat16)


def band_frames(values, tap_table):
    frame_count = values.shape[1]
    reach = BAND // 2
    volume = values.astype(jnp.float32)
    padded = jnp.pad(volume, ((0, 0), (reach, reach), (0, 0), (0, 0)))
    total = volume
    for offset in range(BAND):
        total = total + tap_table[:, offset, None, None, :] * padded[:, offset : offset + frame_count]
    return total.astype(jnp.bfloat16)


def temporal(values, tap_table):
    clip_count, frame_count, pixel_count, channels = values.shape
    groups = lax.axis_size("seq")
    grouped = values.reshape(clip_count, frame_count, groups, pixel_count // groups, channels)
    pixel_view = lax.all_to_all(grouped, "seq", split_axis=2, concat_axis=1, tiled=True)
    pixel_view = pixel_view.reshape(clip_count, groups * frame_count, pixel_count // groups, channels)
    banded = band_frames(pixel_view, tap_table)
    banded = banded.reshape(clip_count, groups * frame_count, 1, pixel_count // groups, channels)
    back = lax.all_to_all(banded, "seq", split_axis=1, concat_axis=2, tiled=True)
    return back.reshape(values.shape)


def temporal_shared(values, tap_table):
    clip_count, frame_count, pixel_count, channels = values.shape
    groups = lax.axis_size("seq")
    planes = lax.axis_size("section")
    grouped = values.reshape(clip_count, frame_count, groups, pixel_count // groups, channels)
    pixel_view = lax.all_to_all(grouped, "seq", split_axis=2, concat_axis=1, tiled=True)
    pixel_view = pixel_view.reshape(clip_count, groups * frame_count, pixel_count // groups, channels)
    banded = band_frames(pixel_view, tap_table)
    banded = jnp.broadcast_to(
        banded[:, None], (clip_count, planes) + banded.shape[1:]
    ).reshape(clip_count, planes * groups * frame_count, 1, pixel_count // groups, channels)
    back = lax.all_to_all(banded, ("section", "seq"), split_axis=1, concat_axis=2, tiled=True)
    back = back.reshape(clip_count, frame_count, planes, pixel_count, channels)
    return jnp.moveaxis(back, 2, 0)


def on_device(clips, cotangent, spatial_taps, modulation, norm_gain, w_in, w_out, band_taps):
    first = lax.axis_index("section") == 0
    taps, mod, gain = spatial_taps[0], modulation[0], norm_gain[0]
    weight_in, weight_out, band = w_in[0], w_out[0], band_taps[0]

    to_first = [(1, 0)]
    core = lax.axis_index("seq") % 2
    siblings = [(q, q ^ 1) for q in range(lax.axis_size("seq"))]

    def fetch_halves(p):
        half = p.shape[0] // 2
        mine = lax.dynamic_slice_in_dim(p, core * half, half, 0)
        got = lax.ppermute(mine, "section", perm=to_first)
        other = lax.ppermute(got, "seq", perm=siblings)
        return jnp.where(core == 0, jnp.concatenate([got, other]), jnp.concatenate([other, got]))

    second_taps, second_mod, second_gain = [
        jnp.where(first, lax.ppermute(p, "section", perm=to_first), p)
        for p in (taps, mod, gain)
    ]
    second_in, second_out = lax.optimization_barrier(
        [jnp.where(first, fetch_halves(p), p) for p in (weight_in, weight_out)]
    )

    first_params = (taps, mod, gain, weight_in, weight_out)
    second_params = (second_taps, second_mod, second_gain, second_in, second_out)

    first_mixed, first_saved = spatial_forward(clips, *first_params)
    lead_in = jnp.where(first, first_mixed, cotangent)
    lead_taps = jnp.where(first, band, band[::-1])
    first_acts, second_seed = temporal_shared(lead_in, lead_taps[None])
    second_mixed, second_saved = spatial_forward(first_acts, *second_params)
    second_grad = spatial_backward(second_saved, second_seed, *second_params)

    tail_in = jnp.where(first, second_grad, second_mixed)
    tail_taps = jnp.where(first, band[::-1], band)
    tail_out = temporal(tail_in, tail_taps[None])
    first_grad = spatial_backward(first_saved, tail_out, *first_params)

    activations = jnp.where(first, first_acts, tail_out)
    input_grads = jnp.where(first, first_grad, second_grad)
    return (activations[None], input_grads[None])


def solution(mesh):
    placed = (
        P(None, "seq", None, None),
        P(None, "seq", None, None),
        P("section", None, None),
        P("section", None, None, None),
        P("section", None),
        P("section", None, None),
        P("section", None, None),
        P("section", None, None),
    )
    return jax.shard_map(
        on_device,
        mesh=mesh,
        in_specs=placed,
        out_specs=(P("section", None, "seq", None, None), P("section", None, "seq", None, None)),
        check_vma=False,
    )
```

```python
import jax
import jax.numpy as jnp
from jax import lax
from jax.sharding import PartitionSpec as P

H = 32
W = 16
BAND = 9


EPSILON = 1e-06


def stencil(volume, stencil_taps):
    zero = ((0, 0), (0, 0))
    padded = jnp.pad(volume, zero + ((1, 1), (0, 0), (0, 0)))
    columns = []
    for across in range(3):
        column = stencil_taps[across] * padded[:, :, 0:H]
        for down_step in range(1, 3):
            column = column + stencil_taps[3 * down_step + across] * padded[:, :, down_step : down_step + H]
        columns.append(column)
    left = jnp.pad(columns[0], zero + ((0, 0), (1, 0), (0, 0)))[:, :, :, :W]
    right = jnp.pad(columns[2], zero + ((0, 0), (0, 1), (0, 0)))[:, :, :, 1:]
    return left + columns[1] + right


def spatial_forward(values, stencil_taps, modulate, norm_gain, w_in, w_out):
    clip_count, frame_count, pixel_count, channels = values.shape
    volume = values.astype(jnp.float32).reshape(clip_count, frame_count, H, W, channels)
    stencil_sum = stencil(volume, stencil_taps).reshape(values.shape)
    scale = (1.0 + modulate[:, 0])[:, None, None, :]
    shift = modulate[:, 1][:, None, None, :]
    modulated = stencil_sum * scale + shift
    inv_rms = lax.rsqrt(jnp.mean(modulated * modulated, axis=-1, keepdims=True) + EPSILON)
    normed = (modulated * inv_rms * norm_gain).astype(jnp.bfloat16).reshape(-1, channels)
    pre = jnp.dot(normed, w_in, preferred_element_type=jnp.float32)
    hidden = jax.nn.silu(pre).astype(jnp.bfloat16)
    update = jnp.dot(hidden, w_out, preferred_element_type=jnp.float32)
    out = (values.astype(jnp.float32) + update.reshape(values.shape)).astype(jnp.bfloat16)
    return out, (modulated, inv_rms, pre)


def spatial_backward(saved, grad, stencil_taps, modulate, norm_gain, w_in, w_out):
    modulated, inv_rms, pre = saved
    clip_count, frame_count, pixel_count, channels = grad.shape
    flat_grad = grad.reshape(-1, channels)
    hidden_grad = jnp.dot(flat_grad, w_out.T, preferred_element_type=jnp.float32).astype(jnp.bfloat16)
    gate = jax.nn.sigmoid(pre)
    pre_grad = hidden_grad.astype(jnp.float32) * (gate * (1.0 + pre * (1.0 - gate)))
    pre_grad = lax.optimization_barrier(pre_grad.astype(jnp.bfloat16))
    normed_grad = jnp.dot(pre_grad, w_in.T, preferred_element_type=jnp.float32).astype(jnp.bfloat16)
    scaled_grad = normed_grad.astype(jnp.float32).reshape(grad.shape) * norm_gain
    inner = jnp.sum(scaled_grad * modulated, axis=-1, keepdims=True)
    modulated_grad = inv_rms * scaled_grad - modulated * (inv_rms * inv_rms * inv_rms) * (inner / channels)
    stencil_grad = modulated_grad * (1.0 + modulate[:, 0])[:, None, None, :]
    spread = stencil(
        stencil_grad.reshape(clip_count, frame_count, H, W, channels), stencil_taps[::-1]
    ).reshape(grad.shape)
    return (grad.astype(jnp.float32) + spread.astype(jnp.bfloat16).astype(jnp.float32)).astype(jnp.bfloat16)


def band_frames(values, tap_table):
    frame_count = values.shape[1]
    reach = BAND // 2
    volume = values.astype(jnp.float32)
    padded = jnp.pad(volume, ((0, 0), (reach, reach), (0, 0), (0, 0)))
    total = volume
    for offset in range(BAND):
        total = total + tap_table[:, offset, None, None, :] * padded[:, offset : offset + frame_count]
    return total.astype(jnp.bfloat16)


def temporal(values, tap_table):
    clip_count, frame_count, pixel_count, channels = values.shape
    groups = lax.axis_size("seq")
    grouped = values.reshape(clip_count, frame_count, groups, pixel_count // groups, channels)
    pixel_view = lax.all_to_all(grouped, "seq", split_axis=2, concat_axis=1, tiled=True)
    pixel_view = pixel_view.reshape(clip_count, groups * frame_count, pixel_count // groups, channels)
    banded = band_frames(pixel_view, tap_table)
    banded = banded.reshape(clip_count, groups * frame_count, 1, pixel_count // groups, channels)
    back = lax.all_to_all(banded, "seq", split_axis=1, concat_axis=2, tiled=True)
    return back.reshape(values.shape)


def temporal_shared(values, tap_table):
    clip_count, frame_count, pixel_count, channels = values.shape
    groups = lax.axis_size("seq")
    planes = lax.axis_size("section")
    grouped = values.reshape(clip_count, frame_count, groups, pixel_count // groups, channels)
    pixel_view = lax.all_to_all(grouped, "seq", split_axis=2, concat_axis=1, tiled=True)
    pixel_view = pixel_view.reshape(clip_count, groups * frame_count, pixel_count // groups, channels)
    banded = band_frames(pixel_view, tap_table)
    banded = jnp.broadcast_to(
        banded[:, None], (clip_count, planes) + banded.shape[1:]
    ).reshape(clip_count, planes * groups * frame_count, 1, pixel_count // groups, channels)
    back = lax.all_to_all(banded, ("section", "seq"), split_axis=1, concat_axis=2, tiled=True)
    back = back.reshape(clip_count, frame_count, planes, pixel_count, channels)
    return jnp.moveaxis(back, 2, 0)


def on_device(clips, cotangent, spatial_taps, modulation, norm_gain, w_in, w_out, band_taps):
    plane = lax.axis_index("section")
    first = plane == 0
    taps, mod, gain = spatial_taps[0], modulation[0], norm_gain[0]
    weight_in, weight_out, band = w_in[0], w_out[0], band_taps[0]
    channels = taps.shape[-1]
    tap_count = taps.shape[0]
    own = (taps, mod, gain, weight_in, weight_out)

    swap = [(0, 1), (1, 0)]
    core = lax.axis_index("seq") % 2
    siblings = [(q, q ^ 1) for q in range(lax.axis_size("seq"))]

    def fetch_halves(p):
        half = p.shape[0] // 2
        mine = lax.dynamic_slice_in_dim(p, core * half, half, 0)
        got = lax.ppermute(mine, "section", perm=swap)
        other = lax.ppermute(got, "seq", perm=siblings)
        return jnp.where(core == 0, jnp.concatenate([got, other]), jnp.concatenate([other, got]))

    small = jnp.concatenate([taps, mod.reshape(-1, channels), gain[None], band])
    got_small = lax.ppermute(small, "section", perm=swap)
    mod_rows = mod.shape[0] * mod.shape[1]
    other = (
        got_small[:tap_count],
        got_small[tap_count : tap_count + mod_rows].reshape(mod.shape),
        got_small[tap_count + mod_rows],
        fetch_halves(weight_in),
        fetch_halves(weight_out),
    )
    other_band = got_small[tap_count + mod_rows + 1 :]
    first_seg = lax.optimization_barrier(
        tuple(jnp.where(first, o, r) for o, r in zip(own, other))
    )
    second_seg = lax.optimization_barrier(
        tuple(jnp.where(first, r, o) for o, r in zip(own, other))
    )
    first_band = jnp.where(first, band, other_band)
    second_band = jnp.where(first, other_band, band)

    def for_clip(params, clip):
        clip_mod = lax.dynamic_index_in_dim(params[1], clip, 0, keepdims=True)
        return (params[0], clip_mod) + tuple(params[2:])

    first_mixed, _ = spatial_forward(clips, *own)
    lead_in = jnp.where(first, first_mixed, cotangent)
    lead_taps = jnp.where(first, band, band[::-1])
    lead_out = temporal(lead_in, lead_taps[None])

    mine = lax.dynamic_index_in_dim(lead_out, plane, 0, keepdims=True)
    theirs = lax.dynamic_index_in_dim(lead_out, 1 - plane, 0, keepdims=True)
    got = lax.ppermute(theirs, "section", perm=swap)
    clip_act = jnp.where(first, mine, got)
    clip_seed = jnp.where(first, got, mine)
    second_params = for_clip(second_seg, plane)
    second_mixed, second_saved = spatial_forward(clip_act, *second_params)
    second_grad = spatial_backward(second_saved, clip_seed, *second_params)

    tail_out = temporal(
        jnp.concatenate([second_grad, second_mixed]), jnp.stack([first_band[::-1], second_band])
    )
    first_params = for_clip(first_seg, plane)
    start = lax.dynamic_index_in_dim(clips, plane, 0, keepdims=True)
    _, first_saved = spatial_forward(start, *first_params)
    first_grad = spatial_backward(first_saved, tail_out[:1], *first_params)

    to_second, to_first = [(0, 1)], [(1, 0)]
    sent_second_grad = lax.ppermute(second_grad, "section", perm=to_second)
    sent_second_act = lax.ppermute(tail_out[1:], "section", perm=to_second)
    sent_first_grad = lax.ppermute(first_grad, "section", perm=to_first)
    activations = jnp.where(
        first, lead_out, jnp.concatenate([sent_second_act, tail_out[1:]])
    )
    input_grads = jnp.where(
        first,
        jnp.concatenate([first_grad, sent_first_grad]),
        jnp.concatenate([sent_second_grad, second_grad]),
    )
    return (activations[None], input_grads[None])


def solution(mesh):
    placed = (
        P(None, "seq", None, None),
        P(None, "seq", None, None),
        P("section", None, None),
        P("section", None, None, None),
        P("section", None),
        P("section", None, None),
        P("section", None, None),
        P("section", None, None),
    )
    return jax.shard_map(
        on_device,
        mesh=mesh,
        in_specs=placed,
        out_specs=(P("section", None, "seq", None, None), P("section", None, "seq", None, None)),
        check_vma=False,
    )
```

```python
import jax
import jax.numpy as jnp
from jax import lax
from jax.sharding import PartitionSpec as P

H = 32
W = 16
BAND = 9


EPSILON = 1e-06


def stencil(volume, stencil_taps):
    zero = ((0, 0), (0, 0))
    padded = jnp.pad(volume, zero + ((1, 1), (0, 0), (0, 0)))
    columns = []
    for across in range(3):
        column = stencil_taps[across] * padded[:, :, 0:H]
        for down_step in range(1, 3):
            column = column + stencil_taps[3 * down_step + across] * padded[:, :, down_step : down_step + H]
        columns.append(column)
    left = jnp.pad(columns[0], zero + ((0, 0), (1, 0), (0, 0)))[:, :, :, :W]
    right = jnp.pad(columns[2], zero + ((0, 0), (0, 1), (0, 0)))[:, :, :, 1:]
    return left + columns[1] + right


def spatial_forward(values, stencil_taps, modulate, norm_gain, w_in, w_out):
    clip_count, frame_count, pixel_count, channels = values.shape
    volume = values.astype(jnp.float32).reshape(clip_count, frame_count, H, W, channels)
    stencil_sum = stencil(volume, stencil_taps).reshape(values.shape)
    scale = (1.0 + modulate[:, 0])[:, None, None, :]
    shift = modulate[:, 1][:, None, None, :]
    modulated = stencil_sum * scale + shift
    inv_rms = lax.rsqrt(jnp.mean(modulated * modulated, axis=-1, keepdims=True) + EPSILON)
    normed = (modulated * inv_rms * norm_gain).astype(jnp.bfloat16).reshape(-1, channels)
    pre = jnp.dot(normed, w_in, preferred_element_type=jnp.float32)
    hidden = jax.nn.silu(pre).astype(jnp.bfloat16)
    update = jnp.dot(hidden, w_out, preferred_element_type=jnp.float32)
    out = (values.astype(jnp.float32) + update.reshape(values.shape)).astype(jnp.bfloat16)
    return out, (modulated, inv_rms, pre)


def spatial_backward(saved, grad, stencil_taps, modulate, norm_gain, w_in, w_out):
    modulated, inv_rms, pre = saved
    clip_count, frame_count, pixel_count, channels = grad.shape
    flat_grad = grad.reshape(-1, channels)
    hidden_grad = jnp.dot(flat_grad, w_out.T, preferred_element_type=jnp.float32).astype(jnp.bfloat16)
    gate = jax.nn.sigmoid(pre)
    pre_grad = hidden_grad.astype(jnp.float32) * (gate * (1.0 + pre * (1.0 - gate)))
    pre_grad = lax.optimization_barrier(pre_grad.astype(jnp.bfloat16))
    normed_grad = jnp.dot(pre_grad, w_in.T, preferred_element_type=jnp.float32).astype(jnp.bfloat16)
    scaled_grad = normed_grad.astype(jnp.float32).reshape(grad.shape) * norm_gain
    inner = jnp.sum(scaled_grad * modulated, axis=-1, keepdims=True)
    modulated_grad = inv_rms * scaled_grad - modulated * (inv_rms * inv_rms * inv_rms) * (inner / channels)
    stencil_grad = modulated_grad * (1.0 + modulate[:, 0])[:, None, None, :]
    spread = stencil(
        stencil_grad.reshape(clip_count, frame_count, H, W, channels), stencil_taps[::-1]
    ).reshape(grad.shape)
    return (grad.astype(jnp.float32) + spread.astype(jnp.bfloat16).astype(jnp.float32)).astype(jnp.bfloat16)


def band_frames(values, tap_table):
    frame_count = values.shape[1]
    reach = BAND // 2
    volume = values.astype(jnp.float32)
    padded = jnp.pad(volume, ((0, 0), (reach, reach), (0, 0), (0, 0)))
    total = volume
    for offset in range(BAND):
        total = total + tap_table[:, offset, None, None, :] * padded[:, offset : offset + frame_count]
    return total.astype(jnp.bfloat16)


def temporal(values, tap_table):
    clip_count, frame_count, pixel_count, channels = values.shape
    groups = lax.axis_size("seq")
    grouped = values.reshape(clip_count, frame_count, groups, pixel_count // groups, channels)
    pixel_view = lax.all_to_all(grouped, "seq", split_axis=2, concat_axis=1, tiled=True)
    pixel_view = pixel_view.reshape(clip_count, groups * frame_count, pixel_count // groups, channels)
    banded = band_frames(pixel_view, tap_table)
    banded = banded.reshape(clip_count, groups * frame_count, 1, pixel_count // groups, channels)
    back = lax.all_to_all(banded, "seq", split_axis=1, concat_axis=2, tiled=True)
    return back.reshape(values.shape)


def temporal_shared(values, tap_table):
    clip_count, frame_count, pixel_count, channels = values.shape
    groups = lax.axis_size("seq")
    planes = lax.axis_size("section")
    grouped = values.reshape(clip_count, frame_count, groups, pixel_count // groups, channels)
    pixel_view = lax.all_to_all(grouped, "seq", split_axis=2, concat_axis=1, tiled=True)
    pixel_view = pixel_view.reshape(clip_count, groups * frame_count, pixel_count // groups, channels)
    banded = band_frames(pixel_view, tap_table)
    banded = jnp.broadcast_to(
        banded[:, None], (clip_count, planes) + banded.shape[1:]
    ).reshape(clip_count, planes * groups * frame_count, 1, pixel_count // groups, channels)
    back = lax.all_to_all(banded, ("section", "seq"), split_axis=1, concat_axis=2, tiled=True)
    back = back.reshape(clip_count, frame_count, planes, pixel_count, channels)
    return jnp.moveaxis(back, 2, 0)


def on_device(clips, cotangent, spatial_taps, modulation, norm_gain, w_in, w_out, band_taps):
    plane = lax.axis_index("section")
    first = plane == 0
    taps, mod, gain = spatial_taps[0], modulation[0], norm_gain[0]
    weight_in, weight_out, band = w_in[0], w_out[0], band_taps[0]
    channels = taps.shape[-1]
    tap_count = taps.shape[0]
    own = (taps, mod, gain, weight_in, weight_out)

    swap = [(0, 1), (1, 0)]
    core = lax.axis_index("seq") % 2
    siblings = [(q, q ^ 1) for q in range(lax.axis_size("seq"))]

    def fetch_halves(p):
        half = p.shape[0] // 2
        mine = lax.dynamic_slice_in_dim(p, core * half, half, 0)
        got = lax.ppermute(mine, "section", perm=swap)
        other = lax.ppermute(got, "seq", perm=siblings)
        return jnp.where(core == 0, jnp.concatenate([got, other]), jnp.concatenate([other, got]))

    small = jnp.concatenate([taps, mod.reshape(-1, channels), gain[None]])
    got_small = lax.ppermute(small, "section", perm=swap)
    mod_rows = mod.shape[0] * mod.shape[1]
    other = (
        got_small[:tap_count],
        got_small[tap_count : tap_count + mod_rows].reshape(mod.shape),
        got_small[tap_count + mod_rows],
        fetch_halves(weight_in),
        fetch_halves(weight_out),
    )
    second_seg = lax.optimization_barrier(
        tuple(jnp.where(first, r, o) for o, r in zip(own, other))
    )

    def for_clip(params, clip):
        clip_mod = lax.dynamic_index_in_dim(params[1], clip, 0, keepdims=True)
        return (params[0], clip_mod) + tuple(params[2:])

    first_mixed, first_saved = spatial_forward(clips, *own)
    lead_in = jnp.where(first, first_mixed, cotangent)
    lead_taps = jnp.where(first, band, band[::-1])
    lead_out = temporal(lead_in, lead_taps[None])

    mine = lax.dynamic_index_in_dim(lead_out, plane, 0, keepdims=True)
    theirs = lax.dynamic_index_in_dim(lead_out, 1 - plane, 0, keepdims=True)
    got = lax.ppermute(theirs, "section", perm=swap)
    clip_act = jnp.where(first, mine, got)
    clip_seed = jnp.where(first, got, mine)
    second_params = for_clip(second_seg, plane)
    second_mixed, second_saved = spatial_forward(clip_act, *second_params)
    second_grad = spatial_backward(second_saved, clip_seed, *second_params)

    got_tail = lax.ppermute(jnp.where(first, second_mixed, second_grad), "section", perm=swap)
    tail_in = jnp.where(
        first,
        jnp.concatenate([second_grad, got_tail]),
        jnp.concatenate([got_tail, second_mixed]),
    )
    tail_taps = jnp.where(first, band[::-1], band)
    tail_out = temporal(tail_in, tail_taps[None])
    first_grad = spatial_backward(first_saved, tail_out, *own)

    sent_second_grad = lax.ppermute(second_grad, "section", perm=[(0, 1)])
    activations = jnp.where(first, lead_out, tail_out)
    input_grads = jnp.where(first, first_grad, jnp.concatenate([sent_second_grad, second_grad]))
    return (activations[None], input_grads[None])


def solution(mesh):
    placed = (
        P(None, "seq", None, None),
        P(None, "seq", None, None),
        P("section", None, None),
        P("section", None, None, None),
        P("section", None),
        P("section", None, None),
        P("section", None, None),
        P("section", None, None),
    )
    return jax.shard_map(
        on_device,
        mesh=mesh,
        in_specs=placed,
        out_specs=(P("section", None, "seq", None, None), P("section", None, "seq", None, None)),
        check_vma=False,
    )
```

```python
import jax
import jax.numpy as jnp
from jax import lax
from jax.sharding import PartitionSpec as P

H = 32
W = 16
BAND = 9


EPSILON = 1e-06


def stencil(volume, stencil_taps):
    zero = ((0, 0), (0, 0))
    padded = jnp.pad(volume, zero + ((1, 1), (0, 0), (0, 0)))
    columns = []
    for across in range(3):
        column = stencil_taps[across] * padded[:, :, 0:H]
        for down_step in range(1, 3):
            column = column + stencil_taps[3 * down_step + across] * padded[:, :, down_step : down_step + H]
        columns.append(column)
    left = jnp.pad(columns[0], zero + ((0, 0), (1, 0), (0, 0)))[:, :, :, :W]
    right = jnp.pad(columns[2], zero + ((0, 0), (0, 1), (0, 0)))[:, :, :, 1:]
    return left + columns[1] + right


def spatial_forward(values, stencil_taps, modulate, norm_gain, w_in, w_out):
    clip_count, frame_count, pixel_count, channels = values.shape
    volume = values.astype(jnp.float32).reshape(clip_count, frame_count, H, W, channels)
    stencil_sum = stencil(volume, stencil_taps).reshape(values.shape)
    scale = (1.0 + modulate[:, 0])[:, None, None, :]
    shift = modulate[:, 1][:, None, None, :]
    modulated = stencil_sum * scale + shift
    inv_rms = lax.rsqrt(jnp.mean(modulated * modulated, axis=-1, keepdims=True) + EPSILON)
    normed = (modulated * inv_rms * norm_gain).astype(jnp.bfloat16).reshape(-1, channels)
    pre = jnp.dot(normed, w_in, preferred_element_type=jnp.float32)
    hidden = jax.nn.silu(pre).astype(jnp.bfloat16)
    update = jnp.dot(hidden, w_out, preferred_element_type=jnp.float32)
    out = (values.astype(jnp.float32) + update.reshape(values.shape)).astype(jnp.bfloat16)
    return out, (modulated, inv_rms, pre)


def spatial_backward(saved, grad, stencil_taps, modulate, norm_gain, w_in, w_out):
    modulated, inv_rms, pre = saved
    clip_count, frame_count, pixel_count, channels = grad.shape
    flat_grad = grad.reshape(-1, channels)
    hidden_grad = jnp.dot(flat_grad, w_out.T, preferred_element_type=jnp.float32).astype(jnp.bfloat16)
    gate = jax.nn.sigmoid(pre)
    pre_grad = hidden_grad.astype(jnp.float32) * (gate * (1.0 + pre * (1.0 - gate)))
    pre_grad = lax.optimization_barrier(pre_grad.astype(jnp.bfloat16))
    normed_grad = jnp.dot(pre_grad, w_in.T, preferred_element_type=jnp.float32).astype(jnp.bfloat16)
    scaled_grad = normed_grad.astype(jnp.float32).reshape(grad.shape) * norm_gain
    inner = jnp.sum(scaled_grad * modulated, axis=-1, keepdims=True)
    modulated_grad = inv_rms * scaled_grad - modulated * (inv_rms * inv_rms * inv_rms) * (inner / channels)
    stencil_grad = modulated_grad * (1.0 + modulate[:, 0])[:, None, None, :]
    spread = stencil(
        stencil_grad.reshape(clip_count, frame_count, H, W, channels), stencil_taps[::-1]
    ).reshape(grad.shape)
    return (grad.astype(jnp.float32) + spread.astype(jnp.bfloat16).astype(jnp.float32)).astype(jnp.bfloat16)


def band_frames(values, tap_table):
    frame_count = values.shape[1]
    reach = BAND // 2
    volume = values.astype(jnp.float32)
    padded = jnp.pad(volume, ((0, 0), (reach, reach), (0, 0), (0, 0)))
    total = volume
    for offset in range(BAND):
        total = total + tap_table[:, offset, None, None, :] * padded[:, offset : offset + frame_count]
    return total.astype(jnp.bfloat16)


def temporal(values, tap_table):
    clip_count, frame_count, pixel_count, channels = values.shape
    groups = lax.axis_size("seq")
    grouped = values.reshape(clip_count, frame_count, groups, pixel_count // groups, channels)
    pixel_view = lax.all_to_all(grouped, "seq", split_axis=2, concat_axis=1, tiled=True)
    pixel_view = pixel_view.reshape(clip_count, groups * frame_count, pixel_count // groups, channels)
    banded = band_frames(pixel_view, tap_table)
    banded = banded.reshape(clip_count, groups * frame_count, 1, pixel_count // groups, channels)
    back = lax.all_to_all(banded, "seq", split_axis=1, concat_axis=2, tiled=True)
    return back.reshape(values.shape)


def temporal_shared(values, tap_table):
    clip_count, frame_count, pixel_count, channels = values.shape
    groups = lax.axis_size("seq")
    planes = lax.axis_size("section")
    grouped = values.reshape(clip_count, frame_count, groups, pixel_count // groups, channels)
    pixel_view = lax.all_to_all(grouped, "seq", split_axis=2, concat_axis=1, tiled=True)
    pixel_view = pixel_view.reshape(clip_count, groups * frame_count, pixel_count // groups, channels)
    banded = band_frames(pixel_view, tap_table)
    banded = jnp.broadcast_to(
        banded[:, None], (clip_count, planes) + banded.shape[1:]
    ).reshape(clip_count, planes * groups * frame_count, 1, pixel_count // groups, channels)
    back = lax.all_to_all(banded, ("section", "seq"), split_axis=1, concat_axis=2, tiled=True)
    back = back.reshape(clip_count, frame_count, planes, pixel_count, channels)
    return jnp.moveaxis(back, 2, 0)


def on_device(clips, cotangent, spatial_taps, modulation, norm_gain, w_in, w_out, band_taps):
    plane = lax.axis_index("section")
    first = plane == 0
    taps, mod, gain = spatial_taps[0], modulation[0], norm_gain[0]
    weight_in, weight_out, band = w_in[0], w_out[0], band_taps[0]
    channels = taps.shape[-1]
    tap_count = taps.shape[0]
    own = (taps, mod, gain, weight_in, weight_out)

    swap = [(0, 1), (1, 0)]
    core = lax.axis_index("seq") % 2
    siblings = [(q, q ^ 1) for q in range(lax.axis_size("seq"))]

    def fetch_halves(p):
        half = p.shape[0] // 2
        mine = lax.dynamic_slice_in_dim(p, core * half, half, 0)
        got = lax.ppermute(mine, "section", perm=swap)
        other = lax.ppermute(got, "seq", perm=siblings)
        return jnp.where(core == 0, jnp.concatenate([got, other]), jnp.concatenate([other, got]))

    small = jnp.concatenate([taps, mod.reshape(-1, channels), gain[None], band])
    got_small = lax.ppermute(small, "section", perm=swap)
    mod_rows = mod.shape[0] * mod.shape[1]
    other = (
        got_small[:tap_count],
        got_small[tap_count : tap_count + mod_rows].reshape(mod.shape),
        got_small[tap_count + mod_rows],
        fetch_halves(weight_in),
        fetch_halves(weight_out),
    )
    other_band = got_small[tap_count + mod_rows + 1 :]
    first_seg = lax.optimization_barrier(
        tuple(jnp.where(first, o, r) for o, r in zip(own, other))
    )
    second_seg = lax.optimization_barrier(
        tuple(jnp.where(first, r, o) for o, r in zip(own, other))
    )
    first_band = jnp.where(first, band, other_band)
    second_band = jnp.where(first, other_band, band)

    def for_clip(params, clip):
        clip_mod = lax.dynamic_index_in_dim(params[1], clip, 0, keepdims=True)
        return (params[0], clip_mod) + tuple(params[2:])

    first_mixed, _ = spatial_forward(clips, *own)
    lead_in = jnp.where(first, first_mixed, cotangent)
    lead_taps = jnp.where(first, band, band[::-1])
    lead_out = temporal(lead_in, lead_taps[None])

    mine = lax.dynamic_index_in_dim(lead_out, plane, 0, keepdims=True)
    theirs = lax.dynamic_index_in_dim(lead_out, 1 - plane, 0, keepdims=True)
    got = lax.ppermute(theirs, "section", perm=swap)
    clip_act = jnp.where(first, mine, got)
    clip_seed = jnp.where(first, got, mine)
    second_params = for_clip(second_seg, plane)
    second_mixed, second_saved = spatial_forward(clip_act, *second_params)
    second_grad = spatial_backward(second_saved, clip_seed, *second_params)

    tail_out = temporal(
        jnp.concatenate([second_grad, second_mixed]), jnp.stack([first_band[::-1], second_band])
    )
    first_params = for_clip(first_seg, plane)
    start = lax.dynamic_index_in_dim(clips, plane, 0, keepdims=True)
    _, first_saved = spatial_forward(start, *first_params)
    first_grad = spatial_backward(first_saved, tail_out[:1], *first_params)

    to_second, to_first = [(0, 1)], [(1, 0)]
    sent_second_grad = lax.ppermute(second_grad, "section", perm=to_second)
    early = lax.optimization_barrier(
        (
            jnp.where(first, lead_out[1:], tail_out[1:]),
            jnp.where(first, first_grad, sent_second_grad),
        )
    )
    sent_second_act = lax.ppermute(tail_out[1:], "section", perm=to_second)
    sent_first_grad = lax.ppermute(first_grad, "section", perm=to_first)
    activations = jnp.concatenate([jnp.where(first, lead_out[:1], sent_second_act), early[0]])
    input_grads = jnp.concatenate([early[1], jnp.where(first, sent_first_grad, second_grad)])
    return (activations[None], input_grads[None])


def solution(mesh):
    placed = (
        P(None, "seq", None, None),
        P(None, "seq", None, None),
        P("section", None, None),
        P("section", None, None, None),
        P("section", None),
        P("section", None, None),
        P("section", None, None),
        P("section", None, None),
    )
    return jax.shard_map(
        on_device,
        mesh=mesh,
        in_specs=placed,
        out_specs=(P("section", None, "seq", None, None), P("section", None, "seq", None, None)),
        check_vma=False,
    )
```

```python
import jax
import jax.numpy as jnp
from jax import lax
from jax.sharding import PartitionSpec as P

H = 32
W = 16
BAND = 9


EPSILON = 1e-06


def stencil(volume, stencil_taps):
    zero = ((0, 0), (0, 0))
    padded = jnp.pad(volume, zero + ((1, 1), (0, 0), (0, 0)))
    columns = []
    for across in range(3):
        column = stencil_taps[across] * padded[:, :, 0:H]
        for down_step in range(1, 3):
            column = column + stencil_taps[3 * down_step + across] * padded[:, :, down_step : down_step + H]
        columns.append(column)
    left = jnp.pad(columns[0], zero + ((0, 0), (1, 0), (0, 0)))[:, :, :, :W]
    right = jnp.pad(columns[2], zero + ((0, 0), (0, 1), (0, 0)))[:, :, :, 1:]
    return left + columns[1] + right


def spatial_forward(values, stencil_taps, modulate, norm_gain, w_in, w_out):
    clip_count, frame_count, pixel_count, channels = values.shape
    volume = values.astype(jnp.float32).reshape(clip_count, frame_count, H, W, channels)
    stencil_sum = stencil(volume, stencil_taps).reshape(values.shape)
    scale = (1.0 + modulate[:, 0])[:, None, None, :]
    shift = modulate[:, 1][:, None, None, :]
    modulated = stencil_sum * scale + shift
    inv_rms = lax.rsqrt(jnp.mean(modulated * modulated, axis=-1, keepdims=True) + EPSILON)
    normed = (modulated * inv_rms * norm_gain).astype(jnp.bfloat16).reshape(-1, channels)
    pre = jnp.dot(normed, w_in, preferred_element_type=jnp.float32)
    hidden = jax.nn.silu(pre).astype(jnp.bfloat16)
    update = jnp.dot(hidden, w_out, preferred_element_type=jnp.float32)
    out = (values.astype(jnp.float32) + update.reshape(values.shape)).astype(jnp.bfloat16)
    return out, (modulated, inv_rms, pre)


def spatial_backward(saved, grad, stencil_taps, modulate, norm_gain, w_in, w_out):
    modulated, inv_rms, pre = saved
    clip_count, frame_count, pixel_count, channels = grad.shape
    flat_grad = grad.reshape(-1, channels)
    hidden_grad = jnp.dot(flat_grad, w_out.T, preferred_element_type=jnp.float32).astype(jnp.bfloat16)
    gate = jax.nn.sigmoid(pre)
    pre_grad = hidden_grad.astype(jnp.float32) * (gate * (1.0 + pre * (1.0 - gate)))
    pre_grad = lax.optimization_barrier(pre_grad.astype(jnp.bfloat16))
    normed_grad = jnp.dot(pre_grad, w_in.T, preferred_element_type=jnp.float32).astype(jnp.bfloat16)
    scaled_grad = normed_grad.astype(jnp.float32).reshape(grad.shape) * norm_gain
    inner = jnp.sum(scaled_grad * modulated, axis=-1, keepdims=True)
    modulated_grad = inv_rms * scaled_grad - modulated * (inv_rms * inv_rms * inv_rms) * (inner / channels)
    stencil_grad = modulated_grad * (1.0 + modulate[:, 0])[:, None, None, :]
    spread = stencil(
        stencil_grad.reshape(clip_count, frame_count, H, W, channels), stencil_taps[::-1]
    ).reshape(grad.shape)
    return (grad.astype(jnp.float32) + spread.astype(jnp.bfloat16).astype(jnp.float32)).astype(jnp.bfloat16)


def band_frames(values, tap_table):
    frame_count = values.shape[1]
    reach = BAND // 2
    volume = values.astype(jnp.float32)
    padded = jnp.pad(volume, ((0, 0), (reach, reach), (0, 0), (0, 0)))
    total = volume
    for offset in range(BAND):
        total = total + tap_table[:, offset, None, None, :] * padded[:, offset : offset + frame_count]
    return total.astype(jnp.bfloat16)


def temporal(values, tap_table):
    clip_count, frame_count, pixel_count, channels = values.shape
    groups = lax.axis_size("seq")
    grouped = values.reshape(clip_count, frame_count, groups, pixel_count // groups, channels)
    pixel_view = lax.all_to_all(grouped, "seq", split_axis=2, concat_axis=1, tiled=True)
    pixel_view = pixel_view.reshape(clip_count, groups * frame_count, pixel_count // groups, channels)
    banded = band_frames(pixel_view, tap_table)
    banded = banded.reshape(clip_count, groups * frame_count, 1, pixel_count // groups, channels)
    back = lax.all_to_all(banded, "seq", split_axis=1, concat_axis=2, tiled=True)
    return back.reshape(values.shape)


def temporal_shared(values, tap_table):
    clip_count, frame_count, pixel_count, channels = values.shape
    groups = lax.axis_size("seq")
    planes = lax.axis_size("section")
    grouped = values.reshape(clip_count, frame_count, groups, pixel_count // groups, channels)
    pixel_view = lax.all_to_all(grouped, "seq", split_axis=2, concat_axis=1, tiled=True)
    pixel_view = pixel_view.reshape(clip_count, groups * frame_count, pixel_count // groups, channels)
    banded = band_frames(pixel_view, tap_table)
    banded = jnp.broadcast_to(
        banded[:, None], (clip_count, planes) + banded.shape[1:]
    ).reshape(clip_count, planes * groups * frame_count, 1, pixel_count // groups, channels)
    back = lax.all_to_all(banded, ("section", "seq"), split_axis=1, concat_axis=2, tiled=True)
    back = back.reshape(clip_count, frame_count, planes, pixel_count, channels)
    return jnp.moveaxis(back, 2, 0)


def temporal_cross(values, tap_table):
    piece_count, frame_count, pixel_count, channels = values.shape
    groups = lax.axis_size("seq")
    grouped = values.reshape(piece_count, frame_count, groups, pixel_count // groups, channels)
    pixel_view = lax.all_to_all(grouped, "seq", split_axis=2, concat_axis=1, tiled=True)
    pixel_view = pixel_view.reshape(piece_count, groups * frame_count, pixel_count // groups, channels)
    banded = band_frames(pixel_view, tap_table)
    banded = banded.reshape(1, piece_count * groups * frame_count, 1, pixel_count // groups, channels)
    back = lax.all_to_all(banded, ("section", "seq"), split_axis=1, concat_axis=2, tiled=True)
    back = back.reshape(frame_count, piece_count, pixel_count, channels)
    return jnp.moveaxis(back, 1, 0)


def on_device(clips, cotangent, spatial_taps, modulation, norm_gain, w_in, w_out, band_taps):
    plane = lax.axis_index("section")
    first = plane == 0
    taps, mod, gain = spatial_taps[0], modulation[0], norm_gain[0]
    weight_in, weight_out, band = w_in[0], w_out[0], band_taps[0]
    channels = taps.shape[-1]
    tap_count = taps.shape[0]
    own = (taps, mod, gain, weight_in, weight_out)

    swap = [(0, 1), (1, 0)]
    core = lax.axis_index("seq") % 2
    siblings = [(q, q ^ 1) for q in range(lax.axis_size("seq"))]

    def fetch_halves(p):
        half = p.shape[0] // 2
        mine = lax.dynamic_slice_in_dim(p, core * half, half, 0)
        got = lax.ppermute(mine, "section", perm=swap)
        other = lax.ppermute(got, "seq", perm=siblings)
        return jnp.where(core == 0, jnp.concatenate([got, other]), jnp.concatenate([other, got]))

    small = jnp.concatenate([taps, mod.reshape(-1, channels), gain[None], band])
    got_small = lax.ppermute(small, "section", perm=swap)
    mod_rows = mod.shape[0] * mod.shape[1]
    other = (
        got_small[:tap_count],
        got_small[tap_count : tap_count + mod_rows].reshape(mod.shape),
        got_small[tap_count + mod_rows],
        fetch_halves(weight_in),
        fetch_halves(weight_out),
    )
    other_band = got_small[tap_count + mod_rows + 1 :]
    second_seg = lax.optimization_barrier(
        tuple(jnp.where(first, r, o) for o, r in zip(own, other))
    )
    first_band = jnp.where(first, band, other_band)
    second_band = jnp.where(first, other_band, band)

    def for_clip(params, clip):
        clip_mod = lax.dynamic_index_in_dim(params[1], clip, 0, keepdims=True)
        return (params[0], clip_mod) + tuple(params[2:])

    first_mixed, first_saved = spatial_forward(clips, *own)
    lead_in = jnp.where(first, first_mixed, cotangent)
    lead_taps = jnp.where(first, band, band[::-1])
    lead_out = temporal(lead_in, lead_taps[None])

    mine = lax.dynamic_index_in_dim(lead_out, plane, 0, keepdims=True)
    theirs = lax.dynamic_index_in_dim(lead_out, 1 - plane, 0, keepdims=True)
    got = lax.ppermute(theirs, "section", perm=swap)
    clip_act = jnp.where(first, mine, got)
    clip_seed = jnp.where(first, got, mine)
    second_params = for_clip(second_seg, plane)
    second_mixed, second_saved = spatial_forward(clip_act, *second_params)
    second_grad = spatial_backward(second_saved, clip_seed, *second_params)

    tail_out = temporal_cross(
        jnp.concatenate([second_grad, second_mixed]), jnp.stack([first_band[::-1], second_band])
    )
    first_grad = spatial_backward(first_saved, tail_out, *own)

    sent_second_grad = lax.ppermute(second_grad, "section", perm=[(0, 1)])
    activations = jnp.where(first, lead_out, tail_out)
    input_grads = jnp.where(first, first_grad, jnp.concatenate([sent_second_grad, second_grad]))
    return (activations[None], input_grads[None])


def solution(mesh):
    placed = (
        P(None, "seq", None, None),
        P(None, "seq", None, None),
        P("section", None, None),
        P("section", None, None, None),
        P("section", None),
        P("section", None, None),
        P("section", None, None),
        P("section", None, None),
    )
    return jax.shard_map(
        on_device,
        mesh=mesh,
        in_specs=placed,
        out_specs=(P("section", None, "seq", None, None), P("section", None, "seq", None, None)),
        check_vma=False,
    )
```

```python
import jax
import jax.numpy as jnp
from jax import lax
from jax.sharding import PartitionSpec as P

H = 32
W = 16
BAND = 9


EPSILON = 1e-06


def stencil(volume, stencil_taps):
    zero = ((0, 0), (0, 0))
    padded = jnp.pad(volume, zero + ((1, 1), (0, 0), (0, 0)))
    columns = []
    for across in range(3):
        column = stencil_taps[across] * padded[:, :, 0:H]
        for down_step in range(1, 3):
            column = column + stencil_taps[3 * down_step + across] * padded[:, :, down_step : down_step + H]
        columns.append(column)
    left = jnp.pad(columns[0], zero + ((0, 0), (1, 0), (0, 0)))[:, :, :, :W]
    right = jnp.pad(columns[2], zero + ((0, 0), (0, 1), (0, 0)))[:, :, :, 1:]
    return left + columns[1] + right


def spatial_forward(values, stencil_taps, modulate, norm_gain, w_in, w_out):
    clip_count, frame_count, pixel_count, channels = values.shape
    volume = values.astype(jnp.float32).reshape(clip_count, frame_count, H, W, channels)
    stencil_sum = stencil(volume, stencil_taps).reshape(values.shape)
    scale = (1.0 + modulate[:, 0])[:, None, None, :]
    shift = modulate[:, 1][:, None, None, :]
    modulated = stencil_sum * scale + shift
    inv_rms = lax.rsqrt(jnp.mean(modulated * modulated, axis=-1, keepdims=True) + EPSILON)
    normed = (modulated * inv_rms * norm_gain).astype(jnp.bfloat16).reshape(-1, channels)
    pre = jnp.dot(normed, w_in, preferred_element_type=jnp.float32)
    hidden = jax.nn.silu(pre).astype(jnp.bfloat16)
    update = jnp.dot(hidden, w_out, preferred_element_type=jnp.float32)
    out = (values.astype(jnp.float32) + update.reshape(values.shape)).astype(jnp.bfloat16)
    return out, (modulated, inv_rms, pre)


def spatial_backward(saved, grad, stencil_taps, modulate, norm_gain, w_in, w_out):
    modulated, inv_rms, pre = saved
    clip_count, frame_count, pixel_count, channels = grad.shape
    flat_grad = grad.reshape(-1, channels)
    hidden_grad = jnp.dot(flat_grad, w_out.T, preferred_element_type=jnp.float32).astype(jnp.bfloat16)
    gate = jax.nn.sigmoid(pre)
    pre_grad = hidden_grad.astype(jnp.float32) * (gate * (1.0 + pre * (1.0 - gate)))
    pre_grad = lax.optimization_barrier(pre_grad.astype(jnp.bfloat16))
    normed_grad = jnp.dot(pre_grad, w_in.T, preferred_element_type=jnp.float32).astype(jnp.bfloat16)
    scaled_grad = normed_grad.astype(jnp.float32).reshape(grad.shape) * norm_gain
    inner = jnp.sum(scaled_grad * modulated, axis=-1, keepdims=True)
    modulated_grad = inv_rms * scaled_grad - modulated * (inv_rms * inv_rms * inv_rms) * (inner / channels)
    stencil_grad = modulated_grad * (1.0 + modulate[:, 0])[:, None, None, :]
    spread = stencil(
        stencil_grad.reshape(clip_count, frame_count, H, W, channels), stencil_taps[::-1]
    ).reshape(grad.shape)
    return (grad.astype(jnp.float32) + spread.astype(jnp.bfloat16).astype(jnp.float32)).astype(jnp.bfloat16)


def band_frames(values, tap_table):
    frame_count = values.shape[1]
    reach = BAND // 2
    volume = values.astype(jnp.float32)
    padded = jnp.pad(volume, ((0, 0), (reach, reach), (0, 0), (0, 0)))
    total = volume
    for offset in range(BAND):
        total = total + tap_table[:, offset, None, None, :] * padded[:, offset : offset + frame_count]
    return total.astype(jnp.bfloat16)


def temporal(values, tap_table):
    clip_count, frame_count, pixel_count, channels = values.shape
    groups = lax.axis_size("seq")
    grouped = values.reshape(clip_count, frame_count, groups, pixel_count // groups, channels)
    pixel_view = lax.all_to_all(grouped, "seq", split_axis=2, concat_axis=1, tiled=True)
    pixel_view = pixel_view.reshape(clip_count, groups * frame_count, pixel_count // groups, channels)
    banded = band_frames(pixel_view, tap_table)
    banded = banded.reshape(clip_count, groups * frame_count, 1, pixel_count // groups, channels)
    back = lax.all_to_all(banded, "seq", split_axis=1, concat_axis=2, tiled=True)
    return back.reshape(values.shape)


def temporal_shared(values, tap_table):
    clip_count, frame_count, pixel_count, channels = values.shape
    groups = lax.axis_size("seq")
    planes = lax.axis_size("section")
    grouped = values.reshape(clip_count, frame_count, groups, pixel_count // groups, channels)
    pixel_view = lax.all_to_all(grouped, "seq", split_axis=2, concat_axis=1, tiled=True)
    pixel_view = pixel_view.reshape(clip_count, groups * frame_count, pixel_count // groups, channels)
    banded = band_frames(pixel_view, tap_table)
    banded = jnp.broadcast_to(
        banded[:, None], (clip_count, planes) + banded.shape[1:]
    ).reshape(clip_count, planes * groups * frame_count, 1, pixel_count // groups, channels)
    back = lax.all_to_all(banded, ("section", "seq"), split_axis=1, concat_axis=2, tiled=True)
    back = back.reshape(clip_count, frame_count, planes, pixel_count, channels)
    return jnp.moveaxis(back, 2, 0)


def temporal_cross(values, tap_table):
    piece_count, frame_count, pixel_count, channels = values.shape
    groups = lax.axis_size("seq")
    grouped = values.reshape(piece_count, frame_count, groups, pixel_count // groups, channels)
    pixel_view = lax.all_to_all(grouped, "seq", split_axis=2, concat_axis=1, tiled=True)
    pixel_view = pixel_view.reshape(piece_count, groups * frame_count, pixel_count // groups, channels)
    banded = band_frames(pixel_view, tap_table)
    banded = banded.reshape(1, piece_count * groups * frame_count, 1, pixel_count // groups, channels)
    back = lax.all_to_all(banded, ("section", "seq"), split_axis=1, concat_axis=2, tiled=True)
    back = back.reshape(frame_count, piece_count, pixel_count, channels)
    return jnp.moveaxis(back, 1, 0)


def on_device(clips, cotangent, spatial_taps, modulation, norm_gain, w_in, w_out, band_taps):
    plane = lax.axis_index("section")
    first = plane == 0
    taps, mod, gain = spatial_taps[0], modulation[0], norm_gain[0]
    weight_in, weight_out, band = w_in[0], w_out[0], band_taps[0]
    channels = taps.shape[-1]
    tap_count = taps.shape[0]
    own = (taps, mod, gain, weight_in, weight_out)

    swap = [(0, 1), (1, 0)]
    core = lax.axis_index("seq") % 2
    siblings = [(q, q ^ 1) for q in range(lax.axis_size("seq"))]

    def fetch_halves(p):
        half = p.shape[0] // 2
        mine = lax.dynamic_slice_in_dim(p, core * half, half, 0)
        got = lax.ppermute(mine, "section", perm=swap)
        other = lax.ppermute(got, "seq", perm=siblings)
        return jnp.where(core == 0, jnp.concatenate([got, other]), jnp.concatenate([other, got]))

    small = jnp.concatenate([taps, mod.reshape(-1, channels), gain[None], band])
    got_small = lax.ppermute(small, "section", perm=swap)
    mod_rows = mod.shape[0] * mod.shape[1]
    other = (
        got_small[:tap_count],
        got_small[tap_count : tap_count + mod_rows].reshape(mod.shape),
        got_small[tap_count + mod_rows],
        fetch_halves(weight_in),
        fetch_halves(weight_out),
    )
    other_band = got_small[tap_count + mod_rows + 1 :]
    second_seg = lax.optimization_barrier(
        tuple(jnp.where(first, r, o) for o, r in zip(own, other))
    )
    first_band = jnp.where(first, band, other_band)
    second_band = jnp.where(first, other_band, band)

    def for_clip(params, clip):
        clip_mod = lax.dynamic_index_in_dim(params[1], clip, 0, keepdims=True)
        return (params[0], clip_mod) + tuple(params[2:])

    first_mixed, first_saved = spatial_forward(clips, *own)
    lead_in = jnp.where(first, first_mixed, cotangent)
    lead_taps = jnp.where(first, band, band[::-1])
    clip_act, clip_seed = temporal_cross(lead_in, lead_taps[None])
    clip_act, clip_seed = clip_act[None], clip_seed[None]
    second_params = for_clip(second_seg, plane)
    second_mixed, second_saved = spatial_forward(clip_act, *second_params)
    second_grad = spatial_backward(second_saved, clip_seed, *second_params)

    tail_out = temporal_cross(
        jnp.concatenate([second_grad, second_mixed]), jnp.stack([first_band[::-1], second_band])
    )
    first_grad = spatial_backward(first_saved, tail_out, *own)

    sent_second_grad = lax.ppermute(second_grad, "section", perm=[(0, 1)])
    other_act = lax.ppermute(clip_act, "section", perm=[(1, 0)])
    activations = jnp.where(first, jnp.concatenate([clip_act, other_act]), tail_out)
    input_grads = jnp.where(first, first_grad, jnp.concatenate([sent_second_grad, second_grad]))
    return (activations[None], input_grads[None])


def solution(mesh):
    placed = (
        P(None, "seq", None, None),
        P(None, "seq", None, None),
        P("section", None, None),
        P("section", None, None, None),
        P("section", None),
        P("section", None, None),
        P("section", None, None),
        P("section", None, None),
    )
    return jax.shard_map(
        on_device,
        mesh=mesh,
        in_specs=placed,
        out_specs=(P("section", None, "seq", None, None), P("section", None, "seq", None, None)),
        check_vma=False,
    )
```

```python
import jax
import jax.numpy as jnp
from jax import lax
from jax.sharding import PartitionSpec as P

H = 32
W = 16
BAND = 9


EPSILON = 1e-06


def stencil(volume, stencil_taps):
    zero = ((0, 0), (0, 0))
    padded = jnp.pad(volume, zero + ((1, 1), (0, 0), (0, 0)))
    columns = []
    for across in range(3):
        column = stencil_taps[across] * padded[:, :, 0:H]
        for down_step in range(1, 3):
            column = column + stencil_taps[3 * down_step + across] * padded[:, :, down_step : down_step + H]
        columns.append(column)
    left = jnp.pad(columns[0], zero + ((0, 0), (1, 0), (0, 0)))[:, :, :, :W]
    right = jnp.pad(columns[2], zero + ((0, 0), (0, 1), (0, 0)))[:, :, :, 1:]
    return left + columns[1] + right


def spatial_forward(values, stencil_taps, modulate, norm_gain, w_in, w_out):
    clip_count, frame_count, pixel_count, channels = values.shape
    volume = values.astype(jnp.float32).reshape(clip_count, frame_count, H, W, channels)
    stencil_sum = stencil(volume, stencil_taps).reshape(values.shape)
    scale = (1.0 + modulate[:, 0])[:, None, None, :]
    shift = modulate[:, 1][:, None, None, :]
    modulated = stencil_sum * scale + shift
    inv_rms = lax.rsqrt(jnp.mean(modulated * modulated, axis=-1, keepdims=True) + EPSILON)
    normed = (modulated * inv_rms * norm_gain).astype(jnp.bfloat16).reshape(-1, channels)
    pre = jnp.dot(normed, w_in, preferred_element_type=jnp.float32)
    hidden = jax.nn.silu(pre).astype(jnp.bfloat16)
    update = jnp.dot(hidden, w_out, preferred_element_type=jnp.float32)
    out = (values.astype(jnp.float32) + update.reshape(values.shape)).astype(jnp.bfloat16)
    return out, (modulated, inv_rms, pre)


def spatial_backward(saved, grad, stencil_taps, modulate, norm_gain, w_in, w_out):
    modulated, inv_rms, pre = saved
    clip_count, frame_count, pixel_count, channels = grad.shape
    flat_grad = grad.reshape(-1, channels)
    hidden_grad = jnp.dot(flat_grad, w_out.T, preferred_element_type=jnp.float32).astype(jnp.bfloat16)
    gate = jax.nn.sigmoid(pre)
    pre_grad = hidden_grad.astype(jnp.float32) * (gate * (1.0 + pre * (1.0 - gate)))
    pre_grad = lax.optimization_barrier(pre_grad.astype(jnp.bfloat16))
    normed_grad = jnp.dot(pre_grad, w_in.T, preferred_element_type=jnp.float32).astype(jnp.bfloat16)
    scaled_grad = normed_grad.astype(jnp.float32).reshape(grad.shape) * norm_gain
    inner = jnp.sum(scaled_grad * modulated, axis=-1, keepdims=True)
    modulated_grad = inv_rms * scaled_grad - modulated * (inv_rms * inv_rms * inv_rms) * (inner / channels)
    stencil_grad = modulated_grad * (1.0 + modulate[:, 0])[:, None, None, :]
    spread = stencil(
        stencil_grad.reshape(clip_count, frame_count, H, W, channels), stencil_taps[::-1]
    ).reshape(grad.shape)
    return (grad.astype(jnp.float32) + spread.astype(jnp.bfloat16).astype(jnp.float32)).astype(jnp.bfloat16)


def band_frames(values, tap_table):
    frame_count = values.shape[1]
    reach = BAND // 2
    volume = values.astype(jnp.float32)
    padded = jnp.pad(volume, ((0, 0), (reach, reach), (0, 0), (0, 0)))
    total = volume
    for offset in range(BAND):
        total = total + tap_table[:, offset, None, None, :] * padded[:, offset : offset + frame_count]
    return total.astype(jnp.bfloat16)


def temporal(values, tap_table):
    clip_count, frame_count, pixel_count, channels = values.shape
    groups = lax.axis_size("seq")
    grouped = values.reshape(clip_count, frame_count, groups, pixel_count // groups, channels)
    pixel_view = lax.all_to_all(grouped, "seq", split_axis=2, concat_axis=1, tiled=True)
    pixel_view = pixel_view.reshape(clip_count, groups * frame_count, pixel_count // groups, channels)
    banded = band_frames(pixel_view, tap_table)
    banded = banded.reshape(clip_count, groups * frame_count, 1, pixel_count // groups, channels)
    back = lax.all_to_all(banded, "seq", split_axis=1, concat_axis=2, tiled=True)
    return back.reshape(values.shape)


def temporal_shared(values, tap_table):
    clip_count, frame_count, pixel_count, channels = values.shape
    groups = lax.axis_size("seq")
    planes = lax.axis_size("section")
    grouped = values.reshape(clip_count, frame_count, groups, pixel_count // groups, channels)
    pixel_view = lax.all_to_all(grouped, "seq", split_axis=2, concat_axis=1, tiled=True)
    pixel_view = pixel_view.reshape(clip_count, groups * frame_count, pixel_count // groups, channels)
    banded = band_frames(pixel_view, tap_table)
    banded = jnp.broadcast_to(
        banded[:, None], (clip_count, planes) + banded.shape[1:]
    ).reshape(clip_count, planes * groups * frame_count, 1, pixel_count // groups, channels)
    back = lax.all_to_all(banded, ("section", "seq"), split_axis=1, concat_axis=2, tiled=True)
    back = back.reshape(clip_count, frame_count, planes, pixel_count, channels)
    return jnp.moveaxis(back, 2, 0)


def temporal_cross(values, tap_table, carried):
    piece_count, frame_count, pixel_count, channels = values.shape
    groups = lax.axis_size("seq")
    grouped = values.reshape(piece_count, frame_count, groups, pixel_count // groups, channels)
    pixel_view = lax.all_to_all(grouped, "seq", split_axis=2, concat_axis=1, tiled=True)
    pixel_view = pixel_view.reshape(piece_count, groups * frame_count, pixel_count // groups, channels)
    pixel_view, carried = lax.optimization_barrier((pixel_view, carried))
    banded = band_frames(pixel_view, tap_table)
    banded = banded.reshape(1, piece_count * groups * frame_count, 1, pixel_count // groups, channels)
    back = lax.all_to_all(banded, ("section", "seq"), split_axis=1, concat_axis=2, tiled=True)
    back = back.reshape(frame_count, piece_count, pixel_count, channels)
    return jnp.moveaxis(back, 1, 0), carried


def on_device(clips, cotangent, spatial_taps, modulation, norm_gain, w_in, w_out, band_taps):
    plane = lax.axis_index("section")
    first = plane == 0
    taps, mod, gain = spatial_taps[0], modulation[0], norm_gain[0]
    weight_in, weight_out, band = w_in[0], w_out[0], band_taps[0]
    channels = taps.shape[-1]
    tap_count = taps.shape[0]
    own = (taps, mod, gain, weight_in, weight_out)

    first_mixed, first_saved = spatial_forward(clips, *own)
    first_mixed, (taps, mod, gain, weight_in, weight_out, band) = lax.optimization_barrier(
        (first_mixed, own + (band,))
    )
    swap = [(0, 1), (1, 0)]
    core = lax.axis_index("seq") % 2
    siblings = [(q, q ^ 1) for q in range(lax.axis_size("seq"))]

    def fetch_halves(p):
        half = p.shape[0] // 2
        mine = lax.dynamic_slice_in_dim(p, core * half, half, 0)
        got = lax.ppermute(mine, "section", perm=swap)
        other = lax.ppermute(got, "seq", perm=siblings)
        return jnp.where(core == 0, jnp.concatenate([got, other]), jnp.concatenate([other, got]))

    small = jnp.concatenate([taps, mod.reshape(-1, channels), gain[None], band])
    got_small = lax.ppermute(small, "section", perm=swap)
    mod_rows = mod.shape[0] * mod.shape[1]
    other = (
        got_small[:tap_count],
        got_small[tap_count : tap_count + mod_rows].reshape(mod.shape),
        got_small[tap_count + mod_rows],
        fetch_halves(weight_in),
        fetch_halves(weight_out),
    )
    other_band = got_small[tap_count + mod_rows + 1 :]
    second_seg = lax.optimization_barrier(
        tuple(jnp.where(first, r, o) for o, r in zip(own, other))
    )
    first_band = jnp.where(first, band, other_band)
    second_band = jnp.where(first, other_band, band)

    def for_clip(params, clip):
        clip_mod = lax.dynamic_index_in_dim(params[1], clip, 0, keepdims=True)
        return (params[0], clip_mod) + tuple(params[2:])

    lead_in = jnp.where(first, first_mixed, cotangent)
    lead_taps = jnp.where(first, band, band[::-1])
    (clip_act, clip_seed), (second_seg, first_band, second_band) = temporal_cross(
        lead_in, lead_taps[None], (second_seg, first_band, second_band)
    )
    clip_act, clip_seed = clip_act[None], clip_seed[None]
    second_params = for_clip(second_seg, plane)
    second_mixed, second_saved = spatial_forward(clip_act, *second_params)
    second_grad = spatial_backward(second_saved, clip_seed, *second_params)

    tail_out, _ = temporal_cross(
        jnp.concatenate([second_grad, second_mixed]), jnp.stack([first_band[::-1], second_band]), ()
    )
    first_grad = spatial_backward(first_saved, tail_out, *own)

    sent_second_grad = lax.ppermute(second_grad, "section", perm=[(0, 1)])
    other_act = lax.ppermute(clip_act, "section", perm=[(1, 0)])
    activations = jnp.where(first, jnp.concatenate([clip_act, other_act]), tail_out)
    input_grads = jnp.where(first, first_grad, jnp.concatenate([sent_second_grad, second_grad]))
    return (activations[None], input_grads[None])


def solution(mesh):
    placed = (
        P(None, "seq", None, None),
        P(None, "seq", None, None),
        P("section", None, None),
        P("section", None, None, None),
        P("section", None),
        P("section", None, None),
        P("section", None, None),
        P("section", None, None),
    )
    return jax.shard_map(
        on_device,
        mesh=mesh,
        in_specs=placed,
        out_specs=(P("section", None, "seq", None, None), P("section", None, "seq", None, None)),
        check_vma=False,
    )
```

```python
import jax
import jax.numpy as jnp
from jax import lax
from jax.sharding import PartitionSpec as P

H = 32
W = 16
BAND = 9


EPSILON = 1e-06


def stencil(volume, stencil_taps):
    zero = ((0, 0), (0, 0))
    padded = jnp.pad(volume, zero + ((1, 1), (0, 0), (0, 0)))
    columns = []
    for across in range(3):
        column = stencil_taps[across] * padded[:, :, 0:H]
        for down_step in range(1, 3):
            column = column + stencil_taps[3 * down_step + across] * padded[:, :, down_step : down_step + H]
        columns.append(column)
    left = jnp.pad(columns[0], zero + ((0, 0), (1, 0), (0, 0)))[:, :, :, :W]
    right = jnp.pad(columns[2], zero + ((0, 0), (0, 1), (0, 0)))[:, :, :, 1:]
    return left + columns[1] + right


def spatial_forward(values, stencil_taps, modulate, norm_gain, w_in, w_out):
    clip_count, frame_count, pixel_count, channels = values.shape
    volume = values.astype(jnp.float32).reshape(clip_count, frame_count, H, W, channels)
    stencil_sum = stencil(volume, stencil_taps).reshape(values.shape)
    scale = (1.0 + modulate[:, 0])[:, None, None, :]
    shift = modulate[:, 1][:, None, None, :]
    modulated = stencil_sum * scale + shift
    inv_rms = lax.rsqrt(jnp.mean(modulated * modulated, axis=-1, keepdims=True) + EPSILON)
    normed = (modulated * inv_rms * norm_gain).astype(jnp.bfloat16).reshape(-1, channels)
    pre = jnp.dot(normed, w_in, preferred_element_type=jnp.float32)
    hidden = jax.nn.silu(pre).astype(jnp.bfloat16)
    update = jnp.dot(hidden, w_out, preferred_element_type=jnp.float32)
    out = (values.astype(jnp.float32) + update.reshape(values.shape)).astype(jnp.bfloat16)
    return out, (modulated, inv_rms, pre)


def silu_slope(saved):
    modulated, inv_rms, pre = saved
    gate = jax.nn.sigmoid(pre)
    return modulated, inv_rms, gate * (1.0 + pre * (1.0 - gate))


def spatial_backward(saved, grad, stencil_taps, modulate, norm_gain, w_in, w_out):
    modulated, inv_rms, slope = saved
    clip_count, frame_count, pixel_count, channels = grad.shape
    flat_grad = grad.reshape(-1, channels)
    hidden_grad = jnp.dot(flat_grad, w_out.T, preferred_element_type=jnp.float32).astype(jnp.bfloat16)
    pre_grad = hidden_grad.astype(jnp.float32) * slope
    pre_grad = lax.optimization_barrier(pre_grad.astype(jnp.bfloat16))
    normed_grad = jnp.dot(pre_grad, w_in.T, preferred_element_type=jnp.float32).astype(jnp.bfloat16)
    scaled_grad = normed_grad.astype(jnp.float32).reshape(grad.shape) * norm_gain
    inner = jnp.sum(scaled_grad * modulated, axis=-1, keepdims=True)
    modulated_grad = inv_rms * scaled_grad - modulated * (inv_rms * inv_rms * inv_rms) * (inner / channels)
    stencil_grad = modulated_grad * (1.0 + modulate[:, 0])[:, None, None, :]
    spread = stencil(
        stencil_grad.reshape(clip_count, frame_count, H, W, channels), stencil_taps[::-1]
    ).reshape(grad.shape)
    return (grad.astype(jnp.float32) + spread.astype(jnp.bfloat16).astype(jnp.float32)).astype(jnp.bfloat16)


def band_frames(values, tap_table):
    frame_count = values.shape[1]
    reach = BAND // 2
    volume = values.astype(jnp.float32)
    padded = jnp.pad(volume, ((0, 0), (reach, reach), (0, 0), (0, 0)))
    total = volume
    for offset in range(BAND):
        total = total + tap_table[:, offset, None, None, :] * padded[:, offset : offset + frame_count]
    return total.astype(jnp.bfloat16)


def temporal(values, tap_table):
    clip_count, frame_count, pixel_count, channels = values.shape
    groups = lax.axis_size("seq")
    grouped = values.reshape(clip_count, frame_count, groups, pixel_count // groups, channels)
    pixel_view = lax.all_to_all(grouped, "seq", split_axis=2, concat_axis=1, tiled=True)
    pixel_view = pixel_view.reshape(clip_count, groups * frame_count, pixel_count // groups, channels)
    banded = band_frames(pixel_view, tap_table)
    banded = banded.reshape(clip_count, groups * frame_count, 1, pixel_count // groups, channels)
    back = lax.all_to_all(banded, "seq", split_axis=1, concat_axis=2, tiled=True)
    return back.reshape(values.shape)


def temporal_shared(values, tap_table):
    clip_count, frame_count, pixel_count, channels = values.shape
    groups = lax.axis_size("seq")
    planes = lax.axis_size("section")
    grouped = values.reshape(clip_count, frame_count, groups, pixel_count // groups, channels)
    pixel_view = lax.all_to_all(grouped, "seq", split_axis=2, concat_axis=1, tiled=True)
    pixel_view = pixel_view.reshape(clip_count, groups * frame_count, pixel_count // groups, channels)
    banded = band_frames(pixel_view, tap_table)
    banded = jnp.broadcast_to(
        banded[:, None], (clip_count, planes) + banded.shape[1:]
    ).reshape(clip_count, planes * groups * frame_count, 1, pixel_count // groups, channels)
    back = lax.all_to_all(banded, ("section", "seq"), split_axis=1, concat_axis=2, tiled=True)
    back = back.reshape(clip_count, frame_count, planes, pixel_count, channels)
    return jnp.moveaxis(back, 2, 0)


def temporal_cross(values, tap_table, carried):
    piece_count, frame_count, pixel_count, channels = values.shape
    groups = lax.axis_size("seq")
    grouped = values.reshape(piece_count, frame_count, groups, pixel_count // groups, channels)
    pixel_view = lax.all_to_all(grouped, "seq", split_axis=2, concat_axis=1, tiled=True)
    pixel_view = pixel_view.reshape(piece_count, groups * frame_count, pixel_count // groups, channels)
    pixel_view, carried = lax.optimization_barrier((pixel_view, carried))
    banded = band_frames(pixel_view, tap_table)
    banded = banded.reshape(1, piece_count * groups * frame_count, 1, pixel_count // groups, channels)
    back = lax.all_to_all(banded, ("section", "seq"), split_axis=1, concat_axis=2, tiled=True)
    back = back.reshape(frame_count, piece_count, pixel_count, channels)
    return jnp.moveaxis(back, 1, 0), carried


def on_device(clips, cotangent, spatial_taps, modulation, norm_gain, w_in, w_out, band_taps):
    plane = lax.axis_index("section")
    first = plane == 0
    taps, mod, gain = spatial_taps[0], modulation[0], norm_gain[0]
    weight_in, weight_out, band = w_in[0], w_out[0], band_taps[0]
    channels = taps.shape[-1]
    tap_count = taps.shape[0]
    own = (taps, mod, gain, weight_in, weight_out)

    first_mixed, first_saved = spatial_forward(clips, *own)
    first_mixed, (taps, mod, gain, weight_in, weight_out, band) = lax.optimization_barrier(
        (first_mixed, own + (band,))
    )
    swap = [(0, 1), (1, 0)]
    core = lax.axis_index("seq") % 2
    siblings = [(q, q ^ 1) for q in range(lax.axis_size("seq"))]

    def fetch_halves(p):
        half = p.shape[0] // 2
        mine = lax.dynamic_slice_in_dim(p, core * half, half, 0)
        got = lax.ppermute(mine, "section", perm=swap)
        other = lax.ppermute(got, "seq", perm=siblings)
        return jnp.where(core == 0, jnp.concatenate([got, other]), jnp.concatenate([other, got]))

    small = jnp.concatenate([taps, mod.reshape(-1, channels), gain[None], band])
    got_small = lax.ppermute(small, "section", perm=swap)
    mod_rows = mod.shape[0] * mod.shape[1]
    other = (
        got_small[:tap_count],
        got_small[tap_count : tap_count + mod_rows].reshape(mod.shape),
        got_small[tap_count + mod_rows],
        fetch_halves(weight_in),
        fetch_halves(weight_out),
    )
    other_band = got_small[tap_count + mod_rows + 1 :]
    second_seg = lax.optimization_barrier(
        tuple(jnp.where(first, r, o) for o, r in zip(own, other))
    )
    first_band = jnp.where(first, band, other_band)
    second_band = jnp.where(first, other_band, band)

    def for_clip(params, clip):
        clip_mod = lax.dynamic_index_in_dim(params[1], clip, 0, keepdims=True)
        return (params[0], clip_mod) + tuple(params[2:])

    lead_in = jnp.where(first, first_mixed, cotangent)
    lead_taps = jnp.where(first, band, band[::-1])
    (clip_act, clip_seed), (second_seg, first_band, second_band) = temporal_cross(
        lead_in, lead_taps[None], (second_seg, first_band, second_band)
    )
    clip_act, clip_seed = clip_act[None], clip_seed[None]
    second_params = for_clip(second_seg, plane)
    second_mixed, second_saved = spatial_forward(clip_act, *second_params)
    second_grad = spatial_backward(silu_slope(second_saved), clip_seed, *second_params)

    tail_out, first_prepared = temporal_cross(
        jnp.concatenate([second_grad, second_mixed]), jnp.stack([first_band[::-1], second_band]), silu_slope(first_saved)
    )
    first_grad = spatial_backward(first_prepared, tail_out, *own)

    sent_second_grad = lax.ppermute(second_grad, "section", perm=[(0, 1)])
    other_act = lax.ppermute(clip_act, "section", perm=[(1, 0)])
    activations = jnp.where(first, jnp.concatenate([clip_act, other_act]), tail_out)
    input_grads = jnp.where(first, first_grad, jnp.concatenate([sent_second_grad, second_grad]))
    return (activations[None], input_grads[None])


def solution(mesh):
    placed = (
        P(None, "seq", None, None),
        P(None, "seq", None, None),
        P("section", None, None),
        P("section", None, None, None),
        P("section", None),
        P("section", None, None),
        P("section", None, None),
        P("section", None, None),
    )
    return jax.shard_map(
        on_device,
        mesh=mesh,
        in_specs=placed,
        out_specs=(P("section", None, "seq", None, None), P("section", None, "seq", None, None)),
        check_vma=False,
    )
```

```python
import jax
import jax.numpy as jnp
from jax import lax
from jax.sharding import PartitionSpec as P

H = 32
W = 16
BAND = 9


EPSILON = 1e-06


def stencil(volume, stencil_taps):
    zero = ((0, 0), (0, 0))
    padded = jnp.pad(volume, zero + ((1, 1), (0, 0), (0, 0)))
    columns = []
    for across in range(3):
        column = stencil_taps[across] * padded[:, :, 0:H]
        for down_step in range(1, 3):
            column = column + stencil_taps[3 * down_step + across] * padded[:, :, down_step : down_step + H]
        columns.append(column)
    left = jnp.pad(columns[0], zero + ((0, 0), (1, 0), (0, 0)))[:, :, :, :W]
    right = jnp.pad(columns[2], zero + ((0, 0), (0, 1), (0, 0)))[:, :, :, 1:]
    return left + columns[1] + right


def spatial_forward(values, stencil_taps, modulate, norm_gain, w_in, w_out):
    clip_count, frame_count, pixel_count, channels = values.shape
    volume = values.astype(jnp.float32).reshape(clip_count, frame_count, H, W, channels)
    stencil_sum = stencil(volume, stencil_taps).reshape(values.shape)
    scale = (1.0 + modulate[:, 0])[:, None, None, :]
    shift = modulate[:, 1][:, None, None, :]
    modulated = stencil_sum * scale + shift
    inv_rms = lax.rsqrt(jnp.mean(modulated * modulated, axis=-1, keepdims=True) + EPSILON)
    normed = (modulated * inv_rms * norm_gain).astype(jnp.bfloat16).reshape(-1, channels)
    pre = jnp.dot(normed, w_in, preferred_element_type=jnp.float32)
    hidden = jax.nn.silu(pre).astype(jnp.bfloat16)
    update = jnp.dot(hidden, w_out, preferred_element_type=jnp.float32)
    out = (values.astype(jnp.float32) + update.reshape(values.shape)).astype(jnp.bfloat16)
    return out, (modulated, inv_rms, pre)


def silu_slope(saved):
    modulated, inv_rms, pre = saved
    gate = jax.nn.sigmoid(pre)
    coefficient = modulated * (inv_rms * inv_rms * inv_rms / modulated.shape[-1])
    return modulated, inv_rms, gate * (1.0 + pre * (1.0 - gate)), coefficient


def spatial_backward(saved, grad, stencil_taps, modulate, norm_gain, w_in, w_out):
    modulated, inv_rms, slope, coefficient = saved
    clip_count, frame_count, pixel_count, channels = grad.shape
    flat_grad = grad.reshape(-1, channels)
    hidden_grad = jnp.dot(flat_grad, w_out.T, preferred_element_type=jnp.float32).astype(jnp.bfloat16)
    pre_grad = hidden_grad.astype(jnp.float32) * slope
    pre_grad = lax.optimization_barrier(pre_grad.astype(jnp.bfloat16))
    normed_grad = jnp.dot(pre_grad, w_in.T, preferred_element_type=jnp.float32).astype(jnp.bfloat16)
    scaled_grad = normed_grad.astype(jnp.float32).reshape(grad.shape) * norm_gain
    inner = jnp.sum(scaled_grad * modulated, axis=-1, keepdims=True)
    modulated_grad = inv_rms * scaled_grad - coefficient * inner
    stencil_grad = modulated_grad * (1.0 + modulate[:, 0])[:, None, None, :]
    spread = stencil(
        stencil_grad.reshape(clip_count, frame_count, H, W, channels), stencil_taps[::-1]
    ).reshape(grad.shape)
    return (grad.astype(jnp.float32) + spread.astype(jnp.bfloat16).astype(jnp.float32)).astype(jnp.bfloat16)


def band_frames(values, tap_table):
    frame_count = values.shape[1]
    reach = BAND // 2
    volume = values.astype(jnp.float32)
    padded = jnp.pad(volume, ((0, 0), (reach, reach), (0, 0), (0, 0)))
    total = volume
    for offset in range(BAND):
        total = total + tap_table[:, offset, None, None, :] * padded[:, offset : offset + frame_count]
    return total.astype(jnp.bfloat16)


def temporal(values, tap_table):
    clip_count, frame_count, pixel_count, channels = values.shape
    groups = lax.axis_size("seq")
    grouped = values.reshape(clip_count, frame_count, groups, pixel_count // groups, channels)
    pixel_view = lax.all_to_all(grouped, "seq", split_axis=2, concat_axis=1, tiled=True)
    pixel_view = pixel_view.reshape(clip_count, groups * frame_count, pixel_count // groups, channels)
    banded = band_frames(pixel_view, tap_table)
    banded = banded.reshape(clip_count, groups * frame_count, 1, pixel_count // groups, channels)
    back = lax.all_to_all(banded, "seq", split_axis=1, concat_axis=2, tiled=True)
    return back.reshape(values.shape)


def temporal_shared(values, tap_table):
    clip_count, frame_count, pixel_count, channels = values.shape
    groups = lax.axis_size("seq")
    planes = lax.axis_size("section")
    grouped = values.reshape(clip_count, frame_count, groups, pixel_count // groups, channels)
    pixel_view = lax.all_to_all(grouped, "seq", split_axis=2, concat_axis=1, tiled=True)
    pixel_view = pixel_view.reshape(clip_count, groups * frame_count, pixel_count // groups, channels)
    banded = band_frames(pixel_view, tap_table)
    banded = jnp.broadcast_to(
        banded[:, None], (clip_count, planes) + banded.shape[1:]
    ).reshape(clip_count, planes * groups * frame_count, 1, pixel_count // groups, channels)
    back = lax.all_to_all(banded, ("section", "seq"), split_axis=1, concat_axis=2, tiled=True)
    back = back.reshape(clip_count, frame_count, planes, pixel_count, channels)
    return jnp.moveaxis(back, 2, 0)


def temporal_cross(values, tap_table, carried):
    piece_count, frame_count, pixel_count, channels = values.shape
    groups = lax.axis_size("seq")
    grouped = values.reshape(piece_count, frame_count, groups, pixel_count // groups, channels)
    pixel_view = lax.all_to_all(grouped, "seq", split_axis=2, concat_axis=1, tiled=True)
    pixel_view = pixel_view.reshape(piece_count, groups * frame_count, pixel_count // groups, channels)
    pixel_view, carried = lax.optimization_barrier((pixel_view, carried))
    banded = band_frames(pixel_view, tap_table)
    banded = banded.reshape(1, piece_count * groups * frame_count, 1, pixel_count // groups, channels)
    back = lax.all_to_all(banded, ("section", "seq"), split_axis=1, concat_axis=2, tiled=True)
    back = back.reshape(frame_count, piece_count, pixel_count, channels)
    return jnp.moveaxis(back, 1, 0), carried


def on_device(clips, cotangent, spatial_taps, modulation, norm_gain, w_in, w_out, band_taps):
    plane = lax.axis_index("section")
    first = plane == 0
    taps, mod, gain = spatial_taps[0], modulation[0], norm_gain[0]
    weight_in, weight_out, band = w_in[0], w_out[0], band_taps[0]
    channels = taps.shape[-1]
    tap_count = taps.shape[0]
    own = (taps, mod, gain, weight_in, weight_out)

    first_mixed, first_saved = spatial_forward(clips, *own)
    first_mixed, (taps, mod, gain, weight_in, weight_out, band) = lax.optimization_barrier(
        (first_mixed, own + (band,))
    )
    swap = [(0, 1), (1, 0)]
    core = lax.axis_index("seq") % 2
    siblings = [(q, q ^ 1) for q in range(lax.axis_size("seq"))]

    def fetch_halves(p):
        half = p.shape[0] // 2
        mine = lax.dynamic_slice_in_dim(p, core * half, half, 0)
        got = lax.ppermute(mine, "section", perm=swap)
        other = lax.ppermute(got, "seq", perm=siblings)
        return jnp.where(core == 0, jnp.concatenate([got, other]), jnp.concatenate([other, got]))

    small = jnp.concatenate([taps, mod.reshape(-1, channels), gain[None], band])
    got_small = lax.ppermute(small, "section", perm=swap)
    mod_rows = mod.shape[0] * mod.shape[1]
    other = (
        got_small[:tap_count],
        got_small[tap_count : tap_count + mod_rows].reshape(mod.shape),
        got_small[tap_count + mod_rows],
        fetch_halves(weight_in),
        fetch_halves(weight_out),
    )
    other_band = got_small[tap_count + mod_rows + 1 :]
    second_seg = lax.optimization_barrier(
        tuple(jnp.where(first, r, o) for o, r in zip(own, other))
    )
    first_band = jnp.where(first, band, other_band)
    second_band = jnp.where(first, other_band, band)

    def for_clip(params, clip):
        clip_mod = lax.dynamic_index_in_dim(params[1], clip, 0, keepdims=True)
        return (params[0], clip_mod) + tuple(params[2:])

    lead_in = jnp.where(first, first_mixed, cotangent)
    lead_taps = jnp.where(first, band, band[::-1])
    (clip_act, clip_seed), (second_seg, first_band, second_band) = temporal_cross(
        lead_in, lead_taps[None], (second_seg, first_band, second_band)
    )
    clip_act, clip_seed = clip_act[None], clip_seed[None]
    second_params = for_clip(second_seg, plane)
    second_mixed, second_saved = spatial_forward(clip_act, *second_params)
    second_grad = spatial_backward(silu_slope(second_saved), clip_seed, *second_params)

    tail_out, first_prepared = temporal_cross(
        jnp.concatenate([second_grad, second_mixed]), jnp.stack([first_band[::-1], second_band]), silu_slope(first_saved)
    )
    first_grad = spatial_backward(first_prepared, tail_out, *own)

    sent_second_grad = lax.ppermute(second_grad, "section", perm=[(0, 1)])
    other_act = lax.ppermute(clip_act, "section", perm=[(1, 0)])
    activations = jnp.where(first, jnp.concatenate([clip_act, other_act]), tail_out)
    input_grads = jnp.where(first, first_grad, jnp.concatenate([sent_second_grad, second_grad]))
    return (activations[None], input_grads[None])


def solution(mesh):
    placed = (
        P(None, "seq", None, None),
        P(None, "seq", None, None),
        P("section", None, None),
        P("section", None, None, None),
        P("section", None),
        P("section", None, None),
        P("section", None, None),
        P("section", None, None),
    )
    return jax.shard_map(
        on_device,
        mesh=mesh,
        in_specs=placed,
        out_specs=(P("section", None, "seq", None, None), P("section", None, "seq", None, None)),
        check_vma=False,
    )
```

```python
import jax
import jax.numpy as jnp
from jax import lax
from jax.sharding import PartitionSpec as P

H = 32
W = 16
BAND = 9


EPSILON = 1e-06


def stencil(volume, stencil_taps):
    zero = ((0, 0), (0, 0))
    padded = jnp.pad(volume, zero + ((1, 1), (0, 0), (0, 0)))
    columns = []
    for across in range(3):
        column = stencil_taps[across] * padded[:, :, 0:H]
        for down_step in range(1, 3):
            column = column + stencil_taps[3 * down_step + across] * padded[:, :, down_step : down_step + H]
        columns.append(column)
    left = jnp.pad(columns[0], zero + ((0, 0), (1, 0), (0, 0)))[:, :, :, :W]
    right = jnp.pad(columns[2], zero + ((0, 0), (0, 1), (0, 0)))[:, :, :, 1:]
    return left + columns[1] + right


def spatial_forward(values, stencil_taps, modulate, norm_gain, w_in, w_out):
    clip_count, frame_count, pixel_count, channels = values.shape
    volume = values.astype(jnp.float32).reshape(clip_count, frame_count, H, W, channels)
    stencil_sum = stencil(volume, stencil_taps).reshape(values.shape)
    scale = (1.0 + modulate[:, 0])[:, None, None, :]
    shift = modulate[:, 1][:, None, None, :]
    modulated = stencil_sum * scale + shift
    inv_rms = lax.rsqrt(jnp.mean(modulated * modulated, axis=-1, keepdims=True) + EPSILON)
    normed = (modulated * inv_rms * norm_gain).astype(jnp.bfloat16).reshape(-1, channels)
    pre = jnp.dot(normed, w_in, preferred_element_type=jnp.float32)
    hidden = jax.nn.silu(pre).astype(jnp.bfloat16)
    update = jnp.dot(hidden, w_out, preferred_element_type=jnp.float32)
    out = (values.astype(jnp.float32) + update.reshape(values.shape)).astype(jnp.bfloat16)
    return out, (modulated, inv_rms, pre)


def silu_slope(saved):
    modulated, inv_rms, pre = saved
    gate = jax.nn.sigmoid(pre)
    return modulated, inv_rms, gate * (1.0 + pre * (1.0 - gate))


def spatial_backward(saved, grad, stencil_taps, modulate, norm_gain, w_in, w_out):
    modulated, inv_rms, slope = saved
    clip_count, frame_count, pixel_count, channels = grad.shape
    flat_grad = grad.reshape(-1, channels)
    hidden_grad = jnp.dot(flat_grad, w_out.T, preferred_element_type=jnp.float32).astype(jnp.bfloat16)
    pre_grad = hidden_grad.astype(jnp.float32) * slope
    pre_grad = lax.optimization_barrier(pre_grad.astype(jnp.bfloat16))
    normed_grad = jnp.dot(pre_grad, w_in.T, preferred_element_type=jnp.float32).astype(jnp.bfloat16)
    scaled_grad = normed_grad.astype(jnp.float32).reshape(grad.shape) * norm_gain
    inner = jnp.sum(scaled_grad * modulated, axis=-1, keepdims=True)
    modulated_grad = inv_rms * scaled_grad - modulated * (inv_rms * inv_rms * inv_rms) * (inner / channels)
    stencil_grad = modulated_grad * (1.0 + modulate[:, 0])[:, None, None, :]
    spread = stencil(
        stencil_grad.reshape(clip_count, frame_count, H, W, channels), stencil_taps[::-1]
    ).reshape(grad.shape)
    return (grad.astype(jnp.float32) + spread.astype(jnp.bfloat16).astype(jnp.float32)).astype(jnp.bfloat16)


def band_frames(values, tap_table):
    frame_count = values.shape[1]
    reach = BAND // 2
    volume = values.astype(jnp.float32)
    padded = jnp.pad(volume, ((0, 0), (reach, reach), (0, 0), (0, 0)))
    total = volume
    for offset in range(BAND):
        total = total + tap_table[:, offset, None, None, :] * padded[:, offset : offset + frame_count]
    return total.astype(jnp.bfloat16)


def temporal(values, tap_table):
    clip_count, frame_count, pixel_count, channels = values.shape
    groups = lax.axis_size("seq")
    grouped = values.reshape(clip_count, frame_count, groups, pixel_count // groups, channels)
    pixel_view = lax.all_to_all(grouped, "seq", split_axis=2, concat_axis=1, tiled=True)
    pixel_view = pixel_view.reshape(clip_count, groups * frame_count, pixel_count // groups, channels)
    banded = band_frames(pixel_view, tap_table)
    banded = banded.reshape(clip_count, groups * frame_count, 1, pixel_count // groups, channels)
    back = lax.all_to_all(banded, "seq", split_axis=1, concat_axis=2, tiled=True)
    return back.reshape(values.shape)


def temporal_shared(values, tap_table):
    clip_count, frame_count, pixel_count, channels = values.shape
    groups = lax.axis_size("seq")
    planes = lax.axis_size("section")
    grouped = values.reshape(clip_count, frame_count, groups, pixel_count // groups, channels)
    pixel_view = lax.all_to_all(grouped, "seq", split_axis=2, concat_axis=1, tiled=True)
    pixel_view = pixel_view.reshape(clip_count, groups * frame_count, pixel_count // groups, channels)
    banded = band_frames(pixel_view, tap_table)
    banded = jnp.broadcast_to(
        banded[:, None], (clip_count, planes) + banded.shape[1:]
    ).reshape(clip_count, planes * groups * frame_count, 1, pixel_count // groups, channels)
    back = lax.all_to_all(banded, ("section", "seq"), split_axis=1, concat_axis=2, tiled=True)
    back = back.reshape(clip_count, frame_count, planes, pixel_count, channels)
    return jnp.moveaxis(back, 2, 0)


def temporal_cross(values, tap_table, carried):
    piece_count, frame_count, pixel_count, channels = values.shape
    groups = lax.axis_size("seq")
    grouped = values.reshape(piece_count, frame_count, groups, pixel_count // groups, channels)
    pixel_view = lax.all_to_all(grouped, "seq", split_axis=2, concat_axis=1, tiled=True)
    pixel_view = pixel_view.reshape(piece_count, groups * frame_count, pixel_count // groups, channels)
    pixel_view, carried = lax.optimization_barrier((pixel_view, carried))
    banded = band_frames(pixel_view, tap_table)
    banded = banded.reshape(1, piece_count * groups * frame_count, 1, pixel_count // groups, channels)
    back = lax.all_to_all(banded, ("section", "seq"), split_axis=1, concat_axis=2, tiled=True)
    back = back.reshape(frame_count, piece_count, pixel_count, channels)
    return jnp.moveaxis(back, 1, 0), carried


def on_device(clips, cotangent, spatial_taps, modulation, norm_gain, w_in, w_out, band_taps):
    plane = lax.axis_index("section")
    first = plane == 0
    taps, mod, gain = spatial_taps[0], modulation[0], norm_gain[0]
    weight_in, weight_out, band = w_in[0], w_out[0], band_taps[0]
    channels = taps.shape[-1]
    tap_count = taps.shape[0]
    own = (taps, mod, gain, weight_in, weight_out)

    first_mixed, _ = spatial_forward(clips, *own)
    first_mixed, (taps, mod, gain, weight_in, weight_out, band) = lax.optimization_barrier(
        (first_mixed, own + (band,))
    )
    swap = [(0, 1), (1, 0)]
    core = lax.axis_index("seq") % 2
    siblings = [(q, q ^ 1) for q in range(lax.axis_size("seq"))]

    def fetch_halves(p):
        half = p.shape[0] // 2
        mine = lax.dynamic_slice_in_dim(p, core * half, half, 0)
        got = lax.ppermute(mine, "section", perm=swap)
        other = lax.ppermute(got, "seq", perm=siblings)
        return jnp.where(core == 0, jnp.concatenate([got, other]), jnp.concatenate([other, got]))

    small = jnp.concatenate([taps, mod.reshape(-1, channels), gain[None], band])
    got_small = lax.ppermute(small, "section", perm=swap)
    mod_rows = mod.shape[0] * mod.shape[1]
    other = (
        got_small[:tap_count],
        got_small[tap_count : tap_count + mod_rows].reshape(mod.shape),
        got_small[tap_count + mod_rows],
        fetch_halves(weight_in),
        fetch_halves(weight_out),
    )
    other_band = got_small[tap_count + mod_rows + 1 :]
    second_seg = lax.optimization_barrier(
        tuple(jnp.where(first, r, o) for o, r in zip(own, other))
    )
    first_band = jnp.where(first, band, other_band)
    second_band = jnp.where(first, other_band, band)

    def for_clip(params, clip):
        clip_mod = lax.dynamic_index_in_dim(params[1], clip, 0, keepdims=True)
        return (params[0], clip_mod) + tuple(params[2:])

    lead_in = jnp.where(first, first_mixed, cotangent)
    lead_taps = jnp.where(first, band, band[::-1])
    (clip_act, clip_seed), (second_seg, first_band, second_band) = temporal_cross(
        lead_in, lead_taps[None], (second_seg, first_band, second_band)
    )
    clip_act, clip_seed = clip_act[None], clip_seed[None]
    again, _ = lax.optimization_barrier((clips, clip_act))
    _, first_saved = spatial_forward(again, *own)
    second_params = for_clip(second_seg, plane)
    second_mixed, second_saved = spatial_forward(clip_act, *second_params)
    second_grad = spatial_backward(silu_slope(second_saved), clip_seed, *second_params)

    tail_out, first_prepared = temporal_cross(
        jnp.concatenate([second_grad, second_mixed]), jnp.stack([first_band[::-1], second_band]), silu_slope(first_saved)
    )
    first_grad = spatial_backward(first_prepared, tail_out, *own)

    sent_second_grad = lax.ppermute(second_grad, "section", perm=[(0, 1)])
    other_act = lax.ppermute(clip_act, "section", perm=[(1, 0)])
    activations = jnp.where(first, jnp.concatenate([clip_act, other_act]), tail_out)
    input_grads = jnp.where(first, first_grad, jnp.concatenate([sent_second_grad, second_grad]))
    return (activations[None], input_grads[None])


def solution(mesh):
    placed = (
        P(None, "seq", None, None),
        P(None, "seq", None, None),
        P("section", None, None),
        P("section", None, None, None),
        P("section", None),
        P("section", None, None),
        P("section", None, None),
        P("section", None, None),
    )
    return jax.shard_map(
        on_device,
        mesh=mesh,
        in_specs=placed,
        out_specs=(P("section", None, "seq", None, None), P("section", None, "seq", None, None)),
        check_vma=False,
    )
```
